32 devices in a mesh: hel: 4 (over y, x), rad: 8 (over z, core).
Axes of the slice: x: 2, y: 2, z: 4, core: 2. Of those that a mesh axis runs over, the one named last changes fastest.
Arguments:
- prev_vector: float32 [16, 256, 16, 512], P('hel', 'rad'), may hold values from -6 to 6
- curr_vector: float32 [16, 256, 16, 512], P('hel', 'rad'), may hold values from -6 to 6
- kinetic_matrix: float32 [256, 256], replicated, may hold values from -0.1875 to 0.1875
- basis_first: float32 [512, 32], replicated, may hold values from -3 to 3
- basis_second: float32 [512, 32], replicated, may hold values from -3 to 3
- chan_table: int32 [512], replicated, may hold values from 0 to 1023, as said below
- potential: float32 [256, 512], P('rad'), may hold values from -0.6 to 0.6
- vib_coupling: float32 [16, 16], replicated, may hold values from -1.5 to 1.5
- vib_energy: float32 [16], replicated, may hold values from -0.4 to 0.4
- coriolis: float32 [16, 512], P('hel'), may hold values from 0.05 to 0.3
- radial_factor: float32 [256], replicated, may hold values from 0.5 to 2
- damping: float32 [256], replicated, may hold values from 0.6 to 1
- stencil: int32 [256], replicated, may hold values from 0 to 252, as said below
- interp_weights: float32 [256, 4], replicated, may hold values from -4 to 4
- frame_rotation: float32 [16, 16], replicated, may hold values from -1.5 to 1.5
Outputs:
- final_vector: float32 [16, 256, 16, 512], P('hel', 'rad')
- product_amp: float32 [16, 256, 16, 512], P('hel', None, None, 'rad')
The draws below stay inside these ranges and needn't reach their ends.
Inputs may be any that keep to these rules, and one draw needn't show every extreme that they name: Values are distinct; channel c pairs level chan_table[c] // 32 of the first diatom with level chan_table[c] % 32 of the second. `stencil`: non-decreasing along the product points, first value 0, last value 256 - 4.
All inputs are finite; a program needn't handle non-finite values.
Results may differ from the reference program's by a relative error of at most 0.0001.
Values sent between devices are 32-bit elements; how exact they have to be, the bound alone decides.
No kernel may reach another device: no remote copies, remote signals or barrier semaphores. Data moves between devices by JAX's collectives and lax.ppermute only.
A program may use at most 128 MiB of HBM per device.

```python
import math
import jax
import jax.numpy as jnp
from jax import lax

K = 16
R = 256
C = 512
V = 16
A = 512
LJ = 32
Q = 256
STEPS = 2


def draw_chan_table(key, part):
    first_key = jax.random.fold_in(key, 11)
    second_key = jax.random.fold_in(key, 23)
    inner = jax.random.permutation(first_key, LJ * LJ - 2)[:C - 2] + 1
    ends = jnp.array([0, LJ * LJ - 1], dtype=jnp.int32)
    values = jnp.concatenate([ends, inner.astype(jnp.int32)])
    return jax.random.permutation(second_key, values).astype(jnp.int32)


def draw_stencil(key, part):
    base = jax.random.randint(jax.random.fold_in(key, 5), (Q - 2,), 0, R - 3)
    middle = jnp.sort(base.astype(jnp.int32))
    first_end = jnp.zeros((1,), dtype=jnp.int32)
    last_end = jnp.full((1,), R - 4, dtype=jnp.int32)
    return jnp.concatenate([first_end, middle, last_end]).astype(jnp.int32)


def steps_of(rng, dims, shards, least, largest):
    level = 1.0
    for axis_at, parts in shards:
        steps = jax.random.uniform(jax.random.fold_in(jax.random.fold_in(rng, 6), axis_at), (parts,), jnp.float32, least / len(shards), largest / len(shards))
        level = level * jnp.repeat(jnp.exp(steps), dims[axis_at] // parts).reshape((-1,) + (1,) * (len(dims) - 1 - axis_at))
    return level


def gaussian(stream_key, shape, spread, limit, split=(), kind=jnp.bfloat16):
    values = spread * jax.random.normal(stream_key, shape, jnp.float32)
    if split:
        values = values * steps_of(stream_key, shape, split, -0.22, 0.18)
    return jnp.clip(values, -limit, limit).astype(kind)


def setup_inputs(seed: int = 0) -> dict:
    streams_of = jax.random.split(jax.random.key(seed), 16)
    prev_vector = gaussian(streams_of[0], (K, R, V, C), 1.0, 6.0, ((0, 4), (1, 8)), jnp.float32)
    curr_vector = gaussian(streams_of[1], (K, R, V, C), 1.0, 6.0, ((0, 4), (1, 8)), jnp.float32)
    kinetic_matrix = gaussian(streams_of[2], (R, R), (4 * R) ** -0.5, 0.1875, (), jnp.float32)
    basis_first = gaussian(streams_of[3], (A, LJ), 0.21, 3.0, (), jnp.float32)
    basis_second = gaussian(streams_of[4], (A, LJ), 0.21, 3.0, (), jnp.float32)
    chan_table = draw_chan_table(jax.random.fold_in(streams_of[15], 71), 0)
    potential = jnp.clip(jax.random.uniform(streams_of[6], (R, A), jnp.float32, -0.6, 0.6) * steps_of(streams_of[6], (R, A), ((0, 8),), -0.4, 0.0), -0.6, 0.6)
    vib_coupling = gaussian(streams_of[7], (V, V), V ** -0.5, 1.5, (), jnp.float32)
    vib_energy = jnp.clip(jax.random.uniform(streams_of[8], (V,), jnp.float32, -0.4, 0.4), -0.4, 0.4)
    coriolis = jnp.clip(jnp.exp(math.log(0.3) - 1.7917595 * jax.random.uniform(streams_of[9], (K, C), jnp.float32) ** steps_of(streams_of[9], (K, C), ((0, 4),), -0.2, 0.2)), 0.05, 0.3)
    radial_factor = jnp.clip(jnp.exp(jax.random.uniform(streams_of[10], (R,), jnp.float32, math.log(0.5), math.log(2.0))), 0.5, 2.0)
    damping = jnp.clip(jax.random.uniform(streams_of[11], (R,), jnp.float32, 0.6, 1.0), 0.6, 1.0)
    stencil = draw_stencil(jax.random.fold_in(streams_of[15], 71), 0)
    interp_weights = gaussian(streams_of[13], (Q, 4), 0.6, 4.0, (), jnp.float32)
    frame_rotation = gaussian(streams_of[14], (K, K), K ** -0.5, 1.5, (), jnp.float32)
    return dict(prev_vector=prev_vector, curr_vector=curr_vector, kinetic_matrix=kinetic_matrix, basis_first=basis_first, basis_second=basis_second, chan_table=chan_table, potential=potential, vib_coupling=vib_coupling, vib_energy=vib_energy, coriolis=coriolis, radial_factor=radial_factor, damping=damping, stencil=stencil, interp_weights=interp_weights, frame_rotation=frame_rotation)


PRECISE = lax.Precision.HIGHEST


def angular_matrix(basis_first, basis_second, chan_table):
    levels = basis_first.shape[1]
    level_grid = jnp.arange(levels, dtype=jnp.int32)
    first_hot = (chan_table[None, :] // levels == level_grid[:, None]).astype(jnp.float32)
    second_hot = (chan_table[None, :] % levels == level_grid[:, None]).astype(jnp.float32)
    first_part = jnp.dot(basis_first, first_hot, precision=PRECISE, preferred_element_type=jnp.float32)
    second_part = jnp.dot(basis_second, second_hot, precision=PRECISE, preferred_element_type=jnp.float32)
    return first_part * second_part


def interp_matrix(stencil, interp_weights, radial_count):
    offsets = jnp.arange(4, dtype=jnp.int32)
    points = jnp.arange(radial_count, dtype=jnp.int32)
    matches = (points[None, None, :] == (stencil[:, None] + offsets[None, :])[:, :, None]).astype(jnp.float32)
    return jnp.sum(matches * interp_weights[:, :, None], axis=1)


def apply_hamiltonian(vector, kinetic_matrix, transform, potential, vib_coupling, vib_energy, coriolis, radial_factor):
    kinetic_part = jnp.einsum('rs,ksvc->krvc', kinetic_matrix, vector, precision=PRECISE, preferred_element_type=jnp.float32)
    flattened = vector.reshape(-1, vector.shape[3])
    angles = jnp.dot(flattened, transform.T, precision=PRECISE, preferred_element_type=jnp.float32)
    angles = angles.reshape(vector.shape[0], vector.shape[1], vector.shape[2], -1)
    angles = jnp.einsum('uv,krva->krua', vib_coupling, angles, precision=PRECISE, preferred_element_type=jnp.float32)
    angles = angles * potential[None, :, None, :]
    angular = jnp.dot(angles.reshape(-1, angles.shape[3]), transform, precision=PRECISE, preferred_element_type=jnp.float32)
    angular = angular.reshape(vector.shape)
    weighted = coriolis[:, None, None, :] * vector
    upper_side = jnp.concatenate([vector[1:], jnp.zeros_like(vector[:1])], axis=0)
    lower_side = jnp.concatenate([jnp.zeros_like(weighted[:1]), weighted[:-1]], axis=0)
    coupled = radial_factor[None, :, None, None] * (coriolis[:, None, None, :] * upper_side + lower_side)
    return kinetic_part + angular + vib_energy[None, None, :, None] * vector + coupled


def reference(prev_vector, curr_vector, kinetic_matrix, basis_first, basis_second, chan_table, potential, vib_coupling, vib_energy, coriolis, radial_factor, damping, stencil, interp_weights, frame_rotation):
    transform = angular_matrix(basis_first, basis_second, chan_table)
    damp_full = damping[None, :, None, None]
    earlier = prev_vector
    current = curr_vector
    for iteration in range(STEPS):
        image = apply_hamiltonian(current, kinetic_matrix, transform, potential, vib_coupling, vib_energy, coriolis, radial_factor)
        following = damp_full * (2.0 * image - damp_full * earlier)
        earlier = current
        current = following
    interp = interp_matrix(stencil, interp_weights, R)
    placed = jnp.einsum('qr,krvc->kqvc', interp, current, precision=PRECISE, preferred_element_type=jnp.float32)
    product_amp = jnp.einsum('jk,kqvc->jqvc', frame_rotation, placed, precision=PRECISE, preferred_element_type=jnp.float32)
    return (current, product_amp)
```

```python
import jax
import jax.numpy as jnp
from jax import lax
from jax.sharding import PartitionSpec as P

STEPS = 2
PRECISE = lax.Precision.HIGHEST


def shifted(block, axis, distance):
    devices = range(lax.axis_size(axis))
    route = [(i - distance, i) for i in devices if i - distance in devices]
    return lax.ppermute(block, axis, route)


def angular_matrix(basis_first, basis_second, chan_table):
    levels = basis_first.shape[1]
    level_grid = jnp.arange(levels, dtype=jnp.int32)
    first_hot = (chan_table[None, :] // levels == level_grid[:, None]).astype(jnp.float32)
    second_hot = (chan_table[None, :] % levels == level_grid[:, None]).astype(jnp.float32)
    first_part = jnp.dot(
        basis_first, first_hot, precision=PRECISE, preferred_element_type=jnp.float32
    )
    second_part = jnp.dot(
        basis_second, second_hot, precision=PRECISE, preferred_element_type=jnp.float32
    )
    return first_part * second_part


def interp_matrix(stencil, interp_weights, radial_count):
    offsets = jnp.arange(4, dtype=jnp.int32)
    points = jnp.arange(radial_count, dtype=jnp.int32)
    matches = (points[None, None, :] == (stencil[:, None] + offsets[None, :])[:, :, None]).astype(
        jnp.float32
    )
    return jnp.sum(matches * interp_weights[:, :, None], axis=1)


def exchange(piece_for, place, out, axis):
    n = lax.axis_size(axis)
    me = lax.axis_index(axis)
    out = place(out, piece_for(me), me)
    for d in range(1, n):
        dest = lax.rem(me + d, n)
        src = lax.rem(me + n - d, n)
        got = lax.ppermute(piece_for(dest), axis, [(i, (i + d) % n) for i in range(n)])
        out = place(out, got, src)
    return out


def shards(
    prev_vector,
    curr_vector,
    kinetic_matrix,
    basis_first,
    basis_second,
    chan_table,
    potential,
    vib_coupling,
    vib_energy,
    coriolis,
    radial_factor,
    damping,
    stencil,
    interp_weights,
    frame_rotation,
):
    kl, rl, vc, cc = curr_vector.shape
    n = lax.axis_size("rad")
    nh = lax.axis_size("hel")
    radial = rl * n
    mb = vc * cc // n
    cb = cc // n
    rad_index = lax.axis_index("rad")
    radial_local = lax.dynamic_slice_in_dim(radial_factor, rad_index * rl, rl)
    damping_local = lax.dynamic_slice_in_dim(damping, rad_index * rl, rl)
    damp_full = damping_local[None, :, None, None]
    transform = angular_matrix(basis_first, basis_second, chan_table)
    vib_batched = jnp.broadcast_to(vib_coupling, (kl * rl, vc, vc))

    def to_radial_columns(x):
        blocks = x.reshape(kl, rl, n, mb)

        def piece_for(dest):
            part = lax.dynamic_index_in_dim(blocks, dest, axis=2, keepdims=False)
            return jnp.transpose(part, (1, 0, 2))

        def place(out, piece, src):
            return lax.dynamic_update_slice_in_dim(out, piece, src * rl, axis=0)

        return exchange(piece_for, place, jnp.zeros((radial, kl, mb), x.dtype), "rad")

    def to_radial_rows(y):
        def piece_for(dest):
            part = lax.dynamic_slice_in_dim(y, dest * rl, rl, axis=0)
            return jnp.transpose(part, (1, 0, 2))

        def place(out, piece, src):
            return lax.dynamic_update_slice_in_dim(out, piece[:, :, None, :], src, axis=2)

        out = exchange(piece_for, place, jnp.zeros((kl, rl, n, mb), y.dtype), "rad")
        return out.reshape(kl, rl, vc, cc)

    def hamiltonian(current):
        columns = to_radial_columns(current)
        applied = jnp.dot(
            kinetic_matrix,
            columns.reshape(radial, kl * mb),
            precision=PRECISE,
            preferred_element_type=jnp.float32,
        )
        kinetic_image = to_radial_rows(applied.reshape(radial, kl, mb))
        angles = jnp.dot(
            current.reshape(-1, cc), transform.T, precision=PRECISE,
            preferred_element_type=jnp.float32,
        )
        angles = jnp.einsum(
            "buv,bva->bua",
            vib_batched,
            angles.reshape(kl * rl, vc, -1),
            precision=PRECISE,
            preferred_element_type=jnp.float32,
        )
        angles = angles.reshape(kl, rl, vc, -1) * potential[None, :, None, :]
        angular = jnp.dot(
            angles.reshape(-1, angles.shape[3]),
            transform,
            precision=PRECISE,
            preferred_element_type=jnp.float32,
        )
        weighted = coriolis[:, None, None, :] * current
        from_above = shifted(current[:1], "hel", -1)
        from_below = shifted(weighted[-1:], "hel", 1)
        upper_side = jnp.concatenate([current[1:], from_above], axis=0)
        lower_side = jnp.concatenate([from_below, weighted[:-1]], axis=0)
        return (
            kinetic_image
            + (angular.reshape(current.shape) + vib_energy[None, None, :, None] * current)
            + radial_local[None, :, None, None]
            * (coriolis[:, None, None, :] * upper_side + lower_side)
        )

    earlier = prev_vector
    current = curr_vector
    for iteration in range(STEPS):
        image = hamiltonian(current)
        following = damp_full * (2.0 * image - damp_full * earlier)
        earlier = current
        current = following

    chans = current.reshape(kl, rl, vc, n, cb)

    def chan_piece(dest):
        part = lax.dynamic_index_in_dim(chans, dest, axis=3, keepdims=False)
        return jnp.transpose(part, (1, 0, 2, 3))

    def chan_place(out, piece, src):
        return lax.dynamic_update_slice_in_dim(out, piece, src * rl, axis=0)

    radial_block = exchange(
        chan_piece, chan_place, jnp.zeros((radial, kl, vc, cb), current.dtype), "rad"
    )
    interp = interp_matrix(stencil, interp_weights, radial)
    qq = interp.shape[0]
    qb = qq // nh
    width = vc * cb
    placed = jnp.dot(
        interp,
        radial_block.reshape(radial, kl * width),
        precision=PRECISE,
        preferred_element_type=jnp.float32,
    ).reshape(qq, kl, width)

    def hel_piece(dest):
        part = lax.dynamic_slice_in_dim(placed, dest * qb, qb, axis=0)
        return jnp.transpose(part, (1, 0, 2))

    def hel_place(out, piece, src):
        return lax.dynamic_update_slice_in_dim(out, piece, src * kl, axis=0)

    gathered = exchange(
        hel_piece, hel_place, jnp.zeros((kl * nh, qb, width), placed.dtype), "hel"
    )
    turned = jnp.dot(
        frame_rotation,
        gathered.reshape(kl * nh, qb * width),
        precision=PRECISE,
        preferred_element_type=jnp.float32,
    ).reshape(kl * nh, qb, width)

    def back_piece(dest):
        return lax.dynamic_slice_in_dim(turned, dest * kl, kl, axis=0)

    def back_place(out, piece, src):
        return lax.dynamic_update_slice_in_dim(out, piece, src * qb, axis=1)

    rotated = exchange(back_piece, back_place, jnp.zeros((kl, qq, width), turned.dtype), "hel")
    product_amp = rotated.reshape(kl, qq, vc, cb)
    return (current, product_amp)


def solution(mesh):
    in_specs = (
        P("hel", "rad", None, None),
        P("hel", "rad", None, None),
        P(),
        P(),
        P(),
        P(),
        P("rad", None),
        P(),
        P(),
        P("hel", None),
        P(),
        P(),
        P(),
        P(),
        P(),
    )
    out_specs = (P("hel", "rad", None, None), P("hel", None, None, "rad"))
    return jax.shard_map(shards, mesh=mesh, in_specs=in_specs, out_specs=out_specs, check_vma=False)
```

```python
import jax
import jax.numpy as jnp
from jax import lax
from jax.sharding import PartitionSpec as P

STEPS = 2
PRECISE = lax.Precision.HIGHEST


def shifted(block, axis, distance):
    devices = range(lax.axis_size(axis))
    route = [(i - distance, i) for i in devices if i - distance in devices]
    return lax.ppermute(block, axis, route)


def angular_matrix(basis_first, basis_second, chan_table):
    levels = basis_first.shape[1]
    level_grid = jnp.arange(levels, dtype=jnp.int32)
    first_hot = (chan_table[None, :] // levels == level_grid[:, None]).astype(jnp.float32)
    second_hot = (chan_table[None, :] % levels == level_grid[:, None]).astype(jnp.float32)
    first_part = jnp.dot(
        basis_first, first_hot, precision=PRECISE, preferred_element_type=jnp.float32
    )
    second_part = jnp.dot(
        basis_second, second_hot, precision=PRECISE, preferred_element_type=jnp.float32
    )
    return first_part * second_part


def interp_matrix(stencil, interp_weights, radial_count):
    offsets = jnp.arange(4, dtype=jnp.int32)
    points = jnp.arange(radial_count, dtype=jnp.int32)
    matches = (points[None, None, :] == (stencil[:, None] + offsets[None, :])[:, :, None]).astype(
        jnp.float32
    )
    return jnp.sum(matches * interp_weights[:, :, None], axis=1)


def shards(
    prev_vector,
    curr_vector,
    kinetic_matrix,
    basis_first,
    basis_second,
    chan_table,
    potential,
    vib_coupling,
    vib_energy,
    coriolis,
    radial_factor,
    damping,
    stencil,
    interp_weights,
    frame_rotation,
):
    kl, rl, vc, cc = curr_vector.shape
    n = lax.axis_size("rad")
    nh = lax.axis_size("hel")
    radial = rl * n
    mb = vc * cc // n
    cb = cc // n
    rad_index = lax.axis_index("rad")
    radial_local = lax.dynamic_slice_in_dim(radial_factor, rad_index * rl, rl)
    damping_local = lax.dynamic_slice_in_dim(damping, rad_index * rl, rl)
    damp_full = damping_local[None, :, None, None]
    transform = angular_matrix(basis_first, basis_second, chan_table)
    vib_batched = jnp.broadcast_to(vib_coupling, (kl * rl, vc, vc))

    kinetic_batched = jnp.broadcast_to(kinetic_matrix, (kl, radial, radial))

    def to_radial_columns(x):
        blocks = jnp.transpose(x.reshape(kl, rl, n, mb), (2, 0, 1, 3))
        got = lax.all_to_all(blocks, "rad", 0, 0, tiled=True).reshape(n, kl, rl, mb)
        return jnp.transpose(got, (1, 0, 2, 3)).reshape(kl, radial, mb)

    def to_radial_rows(y):
        blocks = jnp.transpose(y.reshape(kl, n, rl, mb), (1, 0, 2, 3))
        got = lax.all_to_all(blocks, "rad", 0, 0, tiled=True).reshape(n, kl, rl, mb)
        return jnp.transpose(got, (1, 2, 0, 3)).reshape(kl, rl, vc, cc)

    def hamiltonian(current):
        columns = to_radial_columns(current)
        applied = jnp.einsum(
            "krs,ksm->krm",
            kinetic_batched,
            columns,
            precision=PRECISE,
            preferred_element_type=jnp.float32,
        )
        kinetic_image = to_radial_rows(applied)
        angles = jnp.dot(
            current.reshape(-1, cc), transform.T, precision=PRECISE,
            preferred_element_type=jnp.float32,
        )
        angles = jnp.einsum(
            "buv,bva->bua",
            vib_batched,
            angles.reshape(kl * rl, vc, -1),
            precision=PRECISE,
            preferred_element_type=jnp.float32,
        )
        angles = angles.reshape(kl, rl, vc, -1) * potential[None, :, None, :]
        angular = jnp.dot(
            angles.reshape(-1, angles.shape[3]),
            transform,
            precision=PRECISE,
            preferred_element_type=jnp.float32,
        )
        weighted = coriolis[:, None, None, :] * current
        from_above = shifted(current[:1], "hel", -1)
        from_below = shifted(weighted[-1:], "hel", 1)
        upper_side = jnp.concatenate([current[1:], from_above], axis=0)
        lower_side = jnp.concatenate([from_below, weighted[:-1]], axis=0)
        return (
            kinetic_image
            + (angular.reshape(current.shape) + vib_energy[None, None, :, None] * current)
            + radial_local[None, :, None, None]
            * (coriolis[:, None, None, :] * upper_side + lower_side)
        )

    earlier = prev_vector
    current = curr_vector
    for iteration in range(STEPS):
        image = hamiltonian(current)
        following = damp_full * (2.0 * image - damp_full * earlier)
        earlier = current
        current = following

    width = vc * cb
    chans = jnp.transpose(current.reshape(kl, rl, vc, n, cb), (3, 0, 1, 2, 4))
    got = lax.all_to_all(chans.reshape(n, kl, rl, width), "rad", 0, 0, tiled=True)
    radial_block = jnp.transpose(got.reshape(n, kl, rl, width), (1, 0, 2, 3)).reshape(
        kl, radial, width
    )
    interp = interp_matrix(stencil, interp_weights, radial)
    qq = interp.shape[0]
    qb = qq // nh
    placed = jnp.einsum(
        "kqr,krm->kqm",
        jnp.broadcast_to(interp, (kl, qq, radial)),
        radial_block,
        precision=PRECISE,
        preferred_element_type=jnp.float32,
    )
    pieces = jnp.transpose(placed.reshape(kl, nh, qb, width), (1, 0, 2, 3))
    gathered = lax.all_to_all(pieces, "hel", 0, 0, tiled=True)
    turned = jnp.dot(
        frame_rotation,
        gathered.reshape(nh * kl, qb * width),
        precision=PRECISE,
        preferred_element_type=jnp.float32,
    )
    back = lax.all_to_all(turned.reshape(nh, kl, qb, width), "hel", 0, 0, tiled=True)
    rotated = jnp.transpose(back.reshape(nh, kl, qb, width), (1, 0, 2, 3))
    product_amp = rotated.reshape(kl, qq, vc, cb)
    return (current, product_amp)


def solution(mesh):
    in_specs = (
        P("hel", "rad", None, None),
        P("hel", "rad", None, None),
        P(),
        P(),
        P(),
        P(),
        P("rad", None),
        P(),
        P(),
        P("hel", None),
        P(),
        P(),
        P(),
        P(),
        P(),
    )
    out_specs = (P("hel", "rad", None, None), P("hel", None, None, "rad"))
    return jax.shard_map(shards, mesh=mesh, in_specs=in_specs, out_specs=out_specs, check_vma=False)
```

```python
import jax
import jax.numpy as jnp
from jax import lax
from jax.sharding import PartitionSpec as P

STEPS = 2
PRECISE = lax.Precision.HIGHEST


def shifted(block, axis, distance):
    devices = range(lax.axis_size(axis))
    route = [(i - distance, i) for i in devices if i - distance in devices]
    return lax.ppermute(block, axis, route)


def angular_matrix(basis_first, basis_second, chan_table):
    levels = basis_first.shape[1]
    level_grid = jnp.arange(levels, dtype=jnp.int32)
    first_hot = (chan_table[None, :] // levels == level_grid[:, None]).astype(jnp.float32)
    second_hot = (chan_table[None, :] % levels == level_grid[:, None]).astype(jnp.float32)
    first_part = jnp.dot(
        basis_first, first_hot, precision=PRECISE, preferred_element_type=jnp.float32
    )
    second_part = jnp.dot(
        basis_second, second_hot, precision=PRECISE, preferred_element_type=jnp.float32
    )
    return first_part * second_part


def interp_matrix(stencil, interp_weights, radial_count):
    offsets = jnp.arange(4, dtype=jnp.int32)
    points = jnp.arange(radial_count, dtype=jnp.int32)
    matches = (points[None, None, :] == (stencil[:, None] + offsets[None, :])[:, :, None]).astype(
        jnp.float32
    )
    return jnp.sum(matches * interp_weights[:, :, None], axis=1)


def shards(
    prev_vector,
    curr_vector,
    kinetic_matrix,
    basis_first,
    basis_second,
    chan_table,
    potential,
    vib_coupling,
    vib_energy,
    coriolis,
    radial_factor,
    damping,
    stencil,
    interp_weights,
    frame_rotation,
):
    kl, rl, vc, cc = curr_vector.shape
    n = lax.axis_size("rad")
    nh = lax.axis_size("hel")
    radial = rl * n
    mb = vc * cc // n
    cb = cc // n
    rad_index = lax.axis_index("rad")
    radial_local = lax.dynamic_slice_in_dim(radial_factor, rad_index * rl, rl)
    damping_local = lax.dynamic_slice_in_dim(damping, rad_index * rl, rl)
    damp_full = damping_local[None, :, None, None]
    transform = angular_matrix(basis_first, basis_second, chan_table)
    vib_batched = jnp.broadcast_to(vib_coupling, (kl * rl, vc, vc))

    kinetic_batched = jnp.broadcast_to(kinetic_matrix, (kl, radial, radial))

    def to_radial_columns(x):
        ck = x.shape[0]
        blocks = jnp.transpose(x.reshape(ck, rl, n, mb), (2, 0, 1, 3))
        got = lax.all_to_all(blocks, "rad", 0, 0, tiled=True).reshape(n, ck, rl, mb)
        return jnp.transpose(got, (1, 0, 2, 3)).reshape(ck, radial, mb)

    def to_radial_rows(y):
        ck = y.shape[0]
        blocks = jnp.transpose(y.reshape(ck, n, rl, mb), (1, 0, 2, 3))
        got = lax.all_to_all(blocks, "rad", 0, 0, tiled=True).reshape(n, ck, rl, mb)
        return jnp.transpose(got, (1, 2, 0, 3)).reshape(ck, rl, vc, cc)

    def kinetic(chunk):
        columns = to_radial_columns(chunk)
        applied = jnp.einsum(
            "krs,ksm->krm",
            kinetic_batched[: chunk.shape[0]],
            columns,
            precision=PRECISE,
            preferred_element_type=jnp.float32,
        )
        return to_radial_rows(applied)

    def potential_part(chunk):
        ck = chunk.shape[0]
        angles = jnp.dot(
            chunk.reshape(-1, cc), transform.T, precision=PRECISE,
            preferred_element_type=jnp.float32,
        )
        angles = jnp.einsum(
            "buv,bva->bua",
            vib_batched[: ck * rl],
            angles.reshape(ck * rl, vc, -1),
            precision=PRECISE,
            preferred_element_type=jnp.float32,
        )
        angles = angles.reshape(ck, rl, vc, -1) * potential[None, :, None, :]
        angular = jnp.dot(
            angles.reshape(-1, angles.shape[3]),
            transform,
            precision=PRECISE,
            preferred_element_type=jnp.float32,
        )
        return angular.reshape(chunk.shape) + vib_energy[None, None, :, None] * chunk

    kchunks = 2 if kl % 2 == 0 else 1
    ks = kl // kchunks

    def step(earlier, current):
        whole = jnp.concatenate(current, axis=0)
        weighted = coriolis[:, None, None, :] * whole
        from_above = shifted(whole[:1], "hel", -1)
        from_below = shifted(weighted[-1:], "hel", 1)
        upper_side = jnp.concatenate([whole[1:], from_above], axis=0)
        lower_side = jnp.concatenate([from_below, weighted[:-1]], axis=0)
        following = []
        for i, chunk in enumerate(current):
            sl = slice(i * ks, (i + 1) * ks)
            image = (
                kinetic(chunk)
                + potential_part(chunk)
                + radial_local[None, :, None, None]
                * (coriolis[sl, None, None, :] * upper_side[sl] + lower_side[sl])
            )
            following.append(damp_full * (2.0 * image - damp_full * earlier[i]))
        return following

    def split(x):
        return [x[i * ks:(i + 1) * ks] for i in range(kchunks)]

    earlier = split(prev_vector)
    current = split(curr_vector)
    for iteration in range(STEPS):
        earlier, current = current, step(earlier, current)
    current = jnp.concatenate(current, axis=0)

    interp = interp_matrix(stencil, interp_weights, radial)
    qq = interp.shape[0]
    qb = qq // nh
    interp_batched = jnp.broadcast_to(interp, (kl, qq, radial))
    vchunks = 4 if vc % 4 == 0 else 1
    vs = vc // vchunks
    width = vs * cb
    results = []
    for i in range(vchunks):
        part = current[:, :, i * vs:(i + 1) * vs, :]
        chans = jnp.transpose(part.reshape(kl, rl, vs, n, cb), (3, 0, 1, 2, 4))
        got = lax.all_to_all(chans.reshape(n, kl, rl, width), "rad", 0, 0, tiled=True)
        radial_block = jnp.transpose(got.reshape(n, kl, rl, width), (1, 0, 2, 3)).reshape(
            kl, radial, width
        )
        placed = jnp.einsum(
            "kqr,krm->kqm",
            interp_batched,
            radial_block,
            precision=PRECISE,
            preferred_element_type=jnp.float32,
        )
        pieces = jnp.transpose(placed.reshape(kl, nh, qb, width), (1, 0, 2, 3))
        gathered = lax.all_to_all(pieces, "hel", 0, 0, tiled=True)
        turned = jnp.dot(
            frame_rotation,
            gathered.reshape(nh * kl, qb * width),
            precision=PRECISE,
            preferred_element_type=jnp.float32,
        )
        back = lax.all_to_all(turned.reshape(nh, kl, qb, width), "hel", 0, 0, tiled=True)
        rotated = jnp.transpose(back.reshape(nh, kl, qb, width), (1, 0, 2, 3))
        results.append(rotated.reshape(kl, qq, vs, cb))
    product_amp = jnp.concatenate(results, axis=2)
    return (current, product_amp)


def solution(mesh):
    in_specs = (
        P("hel", "rad", None, None),
        P("hel", "rad", None, None),
        P(),
        P(),
        P(),
        P(),
        P("rad", None),
        P(),
        P(),
        P("hel", None),
        P(),
        P(),
        P(),
        P(),
        P(),
    )
    out_specs = (P("hel", "rad", None, None), P("hel", None, None, "rad"))
    return jax.shard_map(shards, mesh=mesh, in_specs=in_specs, out_specs=out_specs, check_vma=False)
```

```python
import jax
import jax.numpy as jnp
from jax import lax
from jax.sharding import PartitionSpec as P

STEPS = 2
PRECISE = lax.Precision.HIGHEST


def shifted(block, axis, distance):
    devices = range(lax.axis_size(axis))
    route = [(i - distance, i) for i in devices if i - distance in devices]
    return lax.ppermute(block, axis, route)


def angular_matrix(basis_first, basis_second, chan_table):
    levels = basis_first.shape[1]
    level_grid = jnp.arange(levels, dtype=jnp.int32)
    first_hot = (chan_table[None, :] // levels == level_grid[:, None]).astype(jnp.float32)
    second_hot = (chan_table[None, :] % levels == level_grid[:, None]).astype(jnp.float32)
    first_part = jnp.dot(
        basis_first, first_hot, precision=PRECISE, preferred_element_type=jnp.float32
    )
    second_part = jnp.dot(
        basis_second, second_hot, precision=PRECISE, preferred_element_type=jnp.float32
    )
    return first_part * second_part


def interp_matrix(stencil, interp_weights, radial_count):
    offsets = jnp.arange(4, dtype=jnp.int32)
    points = jnp.arange(radial_count, dtype=jnp.int32)
    matches = (points[None, None, :] == (stencil[:, None] + offsets[None, :])[:, :, None]).astype(
        jnp.float32
    )
    return jnp.sum(matches * interp_weights[:, :, None], axis=1)


def shards(
    prev_vector,
    curr_vector,
    kinetic_matrix,
    basis_first,
    basis_second,
    chan_table,
    potential,
    vib_coupling,
    vib_energy,
    coriolis,
    radial_factor,
    damping,
    stencil,
    interp_weights,
    frame_rotation,
):
    kl, rl, vc, cc = curr_vector.shape
    n = lax.axis_size("rad")
    nh = lax.axis_size("hel")
    radial = rl * n
    mb = vc * cc // n
    cb = cc // n
    rad_index = lax.axis_index("rad")
    radial_local = lax.dynamic_slice_in_dim(radial_factor, rad_index * rl, rl)
    damping_local = lax.dynamic_slice_in_dim(damping, rad_index * rl, rl)
    damp_full = damping_local[None, :, None, None]
    transform = angular_matrix(basis_first, basis_second, chan_table)
    vib_batched = jnp.broadcast_to(vib_coupling, (kl * rl, vc, vc))

    kinetic_batched = jnp.broadcast_to(kinetic_matrix, (kl, radial, radial))

    def to_radial_columns(x):
        blocks = jnp.transpose(x.reshape(kl, rl, n, mb), (2, 0, 1, 3))
        got = lax.all_to_all(blocks, "rad", 0, 0, tiled=True).reshape(n, kl, rl, mb)
        return jnp.transpose(got, (1, 0, 2, 3)).reshape(kl, radial, mb)

    def to_radial_rows(y):
        blocks = jnp.transpose(y.reshape(kl, n, rl, mb), (1, 0, 2, 3))
        got = lax.all_to_all(blocks, "rad", 0, 0, tiled=True).reshape(n, kl, rl, mb)
        return jnp.transpose(got, (1, 2, 0, 3)).reshape(kl, rl, vc, cc)

    def hamiltonian(current):
        columns = to_radial_columns(current)
        applied = jnp.einsum(
            "krs,ksm->krm",
            kinetic_batched,
            columns,
            precision=PRECISE,
            preferred_element_type=jnp.float32,
        )
        kinetic_image = to_radial_rows(applied)
        angles = jnp.dot(
            current.reshape(-1, cc), transform.T, precision=PRECISE,
            preferred_element_type=jnp.float32,
        )
        angles = jnp.einsum(
            "buv,bva->bua",
            vib_batched,
            angles.reshape(kl * rl, vc, -1),
            precision=PRECISE,
            preferred_element_type=jnp.float32,
        )
        angles = angles.reshape(kl, rl, vc, -1) * potential[None, :, None, :]
        angular = jnp.dot(
            angles.reshape(-1, angles.shape[3]),
            transform,
            precision=PRECISE,
            preferred_element_type=jnp.float32,
        )
        weighted = coriolis[:, None, None, :] * current
        from_above = shifted(current[:1], "hel", -1)
        from_below = shifted(weighted[-1:], "hel", 1)
        upper_side = jnp.concatenate([current[1:], from_above], axis=0)
        lower_side = jnp.concatenate([from_below, weighted[:-1]], axis=0)
        return (
            kinetic_image
            + (angular.reshape(current.shape) + vib_energy[None, None, :, None] * current)
            + radial_local[None, :, None, None]
            * (coriolis[:, None, None, :] * upper_side + lower_side)
        )

    earlier = prev_vector
    current = curr_vector
    for iteration in range(STEPS):
        image = hamiltonian(current)
        following = damp_full * (2.0 * image - damp_full * earlier)
        earlier = current
        current = following

    hel_index = lax.axis_index("hel")
    interp = interp_matrix(stencil, interp_weights, radial)
    qq = interp.shape[0]
    qb = qq // nh
    turn = jnp.arange(nh, dtype=jnp.int32)
    q_rows = (lax.rem(hel_index + turn, nh)[:, None] * qb + jnp.arange(qb)[None, :]).reshape(-1)
    interp_turned = jnp.broadcast_to(interp[q_rows], (kl, qq, radial))
    k_cols = (lax.rem(hel_index - turn + nh, nh)[:, None] * kl + jnp.arange(kl)[None, :]).reshape(-1)
    j_rows = (lax.rem(hel_index + turn, nh)[:, None] * kl + jnp.arange(kl)[None, :]).reshape(-1)
    frame_turned = frame_rotation[j_rows][:, k_cols]

    def hel_shift(x, d):
        if d == 0:
            return x
        return lax.ppermute(x, "hel", [(i, (i + d) % nh) for i in range(nh)])

    vchunks = 4 if vc % 4 == 0 else 1
    vs = vc // vchunks
    width = vs * cb
    results = []
    for i in range(vchunks):
        part = current[:, :, i * vs:(i + 1) * vs, :]
        chans = jnp.transpose(part.reshape(kl, rl, vs, n, cb), (3, 0, 1, 2, 4))
        got = lax.all_to_all(chans.reshape(n, kl, rl, width), "rad", 0, 0, tiled=True)
        radial_block = jnp.transpose(got.reshape(n, kl, rl, width), (1, 0, 2, 3)).reshape(
            kl, radial, width
        )
        placed = jnp.einsum(
            "kqr,krm->kqm",
            interp_turned,
            radial_block,
            precision=PRECISE,
            preferred_element_type=jnp.float32,
        )
        arrived = [hel_shift(placed[:, d * qb:(d + 1) * qb], d) for d in range(nh)]
        gathered = jnp.stack(arrived, axis=0)
        turned = jnp.dot(
            frame_turned,
            gathered.reshape(nh * kl, qb * width),
            precision=PRECISE,
            preferred_element_type=jnp.float32,
        ).reshape(nh, kl, qb, width)
        back = [hel_shift(turned[e], e) for e in range(nh)]
        blocks = []
        for block in range(nh):
            source = lax.rem(hel_index - block + nh, nh)
            pick = back[0]
            for e in range(1, nh):
                pick = jnp.where(source == e, back[e], pick)
            blocks.append(pick)
        rotated = jnp.concatenate(blocks, axis=1)
        results.append(rotated.reshape(kl, qq, vs, cb))
    product_amp = jnp.concatenate(results, axis=2)
    return (current, product_amp)


def solution(mesh):
    in_specs = (
        P("hel", "rad", None, None),
        P("hel", "rad", None, None),
        P(),
        P(),
        P(),
        P(),
        P("rad", None),
        P(),
        P(),
        P("hel", None),
        P(),
        P(),
        P(),
        P(),
        P(),
    )
    out_specs = (P("hel", "rad", None, None), P("hel", None, None, "rad"))
    return jax.shard_map(shards, mesh=mesh, in_specs=in_specs, out_specs=out_specs, check_vma=False)
```

```python
import jax
import jax.numpy as jnp
from jax import lax
from jax.sharding import PartitionSpec as P

STEPS = 2
PRECISE = lax.Precision.HIGHEST


def shifted(block, axis, distance):
    devices = range(lax.axis_size(axis))
    route = [(i - distance, i) for i in devices if i - distance in devices]
    return lax.ppermute(block, axis, route)


def angular_matrix(basis_first, basis_second, chan_table):
    levels = basis_first.shape[1]
    level_grid = jnp.arange(levels, dtype=jnp.int32)
    first_hot = (chan_table[None, :] // levels == level_grid[:, None]).astype(jnp.float32)
    second_hot = (chan_table[None, :] % levels == level_grid[:, None]).astype(jnp.float32)
    first_part = jnp.dot(
        basis_first, first_hot, precision=PRECISE, preferred_element_type=jnp.float32
    )
    second_part = jnp.dot(
        basis_second, second_hot, precision=PRECISE, preferred_element_type=jnp.float32
    )
    return first_part * second_part


def interp_matrix(stencil, interp_weights, radial_count):
    offsets = jnp.arange(4, dtype=jnp.int32)
    points = jnp.arange(radial_count, dtype=jnp.int32)
    matches = (points[None, None, :] == (stencil[:, None] + offsets[None, :])[:, :, None]).astype(
        jnp.float32
    )
    return jnp.sum(matches * interp_weights[:, :, None], axis=1)


def shards(
    prev_vector,
    curr_vector,
    kinetic_matrix,
    basis_first,
    basis_second,
    chan_table,
    potential,
    vib_coupling,
    vib_energy,
    coriolis,
    radial_factor,
    damping,
    stencil,
    interp_weights,
    frame_rotation,
):
    kl, rl, vc, cc = curr_vector.shape
    n = lax.axis_size("rad")
    nh = lax.axis_size("hel")
    radial = rl * n
    mb = vc * cc // n
    cb = cc // n
    rad_index = lax.axis_index("rad")
    radial_local = lax.dynamic_slice_in_dim(radial_factor, rad_index * rl, rl)
    damping_local = lax.dynamic_slice_in_dim(damping, rad_index * rl, rl)
    damp_full = damping_local[None, :, None, None]
    transform = angular_matrix(basis_first, basis_second, chan_table)
    vib_batched = jnp.broadcast_to(vib_coupling, (kl * rl, vc, vc))

    kinetic_batched = jnp.broadcast_to(kinetic_matrix, (kl, radial, radial))

    def to_radial_columns(x):
        blocks = jnp.transpose(x.reshape(kl, rl, n, mb), (2, 0, 1, 3))
        got = lax.all_to_all(blocks, "rad", 0, 0, tiled=True).reshape(n, kl, rl, mb)
        return jnp.transpose(got, (1, 0, 2, 3)).reshape(kl, radial, mb)

    def to_radial_rows(y):
        blocks = jnp.transpose(y.reshape(kl, n, rl, mb), (1, 0, 2, 3))
        got = lax.all_to_all(blocks, "rad", 0, 0, tiled=True).reshape(n, kl, rl, mb)
        return jnp.transpose(got, (1, 2, 0, 3)).reshape(kl, rl, vc, cc)

    def kinetic(columns):
        return jnp.einsum(
            "krs,ksm->krm",
            kinetic_batched,
            columns,
            precision=PRECISE,
            preferred_element_type=jnp.float32,
        )

    def local_part(current):
        angles = jnp.dot(
            current.reshape(-1, cc), transform.T, precision=PRECISE,
            preferred_element_type=jnp.float32,
        )
        angles = jnp.einsum(
            "buv,bva->bua",
            vib_batched,
            angles.reshape(kl * rl, vc, -1),
            precision=PRECISE,
            preferred_element_type=jnp.float32,
        )
        angles = angles.reshape(kl, rl, vc, -1) * potential[None, :, None, :]
        angular = jnp.dot(
            angles.reshape(-1, angles.shape[3]),
            transform,
            precision=PRECISE,
            preferred_element_type=jnp.float32,
        )
        weighted = coriolis[:, None, None, :] * current
        from_above = shifted(current[:1], "hel", -1)
        from_below = shifted(weighted[-1:], "hel", 1)
        upper_side = jnp.concatenate([current[1:], from_above], axis=0)
        lower_side = jnp.concatenate([from_below, weighted[:-1]], axis=0)
        return (
            angular.reshape(current.shape) + vib_energy[None, None, :, None] * current
        ) + radial_local[None, :, None, None] * (
            coriolis[:, None, None, :] * upper_side + lower_side
        )

    damp_columns = damping[None, :, None]
    earlier = prev_vector
    current = curr_vector
    columns = to_radial_columns(current)
    for iteration in range(STEPS - 1):
        rest = damp_full * (2.0 * local_part(current) - damp_full * earlier)
        following_columns = damp_columns * (2.0 * kinetic(columns)) + to_radial_columns(rest)
        earlier = current
        current = to_radial_rows(following_columns)
        columns = following_columns
    kinetic_image = to_radial_rows(kinetic(columns))
    image = kinetic_image + local_part(current)
    current = damp_full * (2.0 * image - damp_full * earlier)

    hel_index = lax.axis_index("hel")
    interp = interp_matrix(stencil, interp_weights, radial)
    qq = interp.shape[0]
    qb = qq // nh
    turn = jnp.arange(nh, dtype=jnp.int32)
    q_rows = (lax.rem(hel_index + turn, nh)[:, None] * qb + jnp.arange(qb)[None, :]).reshape(-1)
    interp_turned = jnp.broadcast_to(interp[q_rows], (kl, qq, radial))
    k_cols = (lax.rem(hel_index - turn + nh, nh)[:, None] * kl + jnp.arange(kl)[None, :]).reshape(-1)
    j_rows = (lax.rem(hel_index + turn, nh)[:, None] * kl + jnp.arange(kl)[None, :]).reshape(-1)
    frame_turned = frame_rotation[j_rows][:, k_cols]

    def hel_shift(x, d):
        if d == 0:
            return x
        return lax.ppermute(x, "hel", [(i, (i + d) % nh) for i in range(nh)])

    vchunks = 4 if vc % 4 == 0 else 1
    vs = vc // vchunks
    width = vs * cb
    results = []
    for i in range(vchunks):
        part = current[:, :, i * vs:(i + 1) * vs, :]
        chans = jnp.transpose(part.reshape(kl, rl, vs, n, cb), (3, 0, 1, 2, 4))
        got = lax.all_to_all(chans.reshape(n, kl, rl, width), "rad", 0, 0, tiled=True)
        radial_block = jnp.transpose(got.reshape(n, kl, rl, width), (1, 0, 2, 3)).reshape(
            kl, radial, width
        )
        placed = jnp.einsum(
            "kqr,krm->kqm",
            interp_turned,
            radial_block,
            precision=PRECISE,
            preferred_element_type=jnp.float32,
        )
        arrived = [hel_shift(placed[:, d * qb:(d + 1) * qb], d) for d in range(nh)]
        gathered = jnp.stack(arrived, axis=0)
        turned = jnp.dot(
            frame_turned,
            gathered.reshape(nh * kl, qb * width),
            precision=PRECISE,
            preferred_element_type=jnp.float32,
        ).reshape(nh, kl, qb, width)
        back = [hel_shift(turned[e], e) for e in range(nh)]
        blocks = []
        for block in range(nh):
            source = lax.rem(hel_index - block + nh, nh)
            pick = back[0]
            for e in range(1, nh):
                pick = jnp.where(source == e, back[e], pick)
            blocks.append(pick)
        rotated = jnp.concatenate(blocks, axis=1)
        results.append(rotated.reshape(kl, qq, vs, cb))
    product_amp = jnp.concatenate(results, axis=2)
    return (current, product_amp)


def solution(mesh):
    in_specs = (
        P("hel", "rad", None, None),
        P("hel", "rad", None, None),
        P(),
        P(),
        P(),
        P(),
        P("rad", None),
        P(),
        P(),
        P("hel", None),
        P(),
        P(),
        P(),
        P(),
        P(),
    )
    out_specs = (P("hel", "rad", None, None), P("hel", None, None, "rad"))
    return jax.shard_map(shards, mesh=mesh, in_specs=in_specs, out_specs=out_specs, check_vma=False)
```

```python
import jax
import jax.numpy as jnp
from jax import lax
from jax.sharding import PartitionSpec as P

STEPS = 2
PRECISE = lax.Precision.HIGHEST


def shifted(block, axis, distance):
    devices = range(lax.axis_size(axis))
    route = [(i - distance, i) for i in devices if i - distance in devices]
    return lax.ppermute(block, axis, route)


def angular_matrix(basis_first, basis_second, chan_table):
    levels = basis_first.shape[1]
    level_grid = jnp.arange(levels, dtype=jnp.int32)
    first_hot = (chan_table[None, :] // levels == level_grid[:, None]).astype(jnp.float32)
    second_hot = (chan_table[None, :] % levels == level_grid[:, None]).astype(jnp.float32)
    first_part = jnp.dot(
        basis_first, first_hot, precision=PRECISE, preferred_element_type=jnp.float32
    )
    second_part = jnp.dot(
        basis_second, second_hot, precision=PRECISE, preferred_element_type=jnp.float32
    )
    return first_part * second_part


def interp_matrix(stencil, interp_weights, radial_count):
    offsets = jnp.arange(4, dtype=jnp.int32)
    points = jnp.arange(radial_count, dtype=jnp.int32)
    matches = (points[None, None, :] == (stencil[:, None] + offsets[None, :])[:, :, None]).astype(
        jnp.float32
    )
    return jnp.sum(matches * interp_weights[:, :, None], axis=1)


def shards(
    prev_vector,
    curr_vector,
    kinetic_matrix,
    basis_first,
    basis_second,
    chan_table,
    potential,
    vib_coupling,
    vib_energy,
    coriolis,
    radial_factor,
    damping,
    stencil,
    interp_weights,
    frame_rotation,
):
    kl, rl, vc, cc = curr_vector.shape
    n = lax.axis_size("rad")
    nh = lax.axis_size("hel")
    radial = rl * n
    mb = vc * cc // n
    cb = cc // n
    rad_index = lax.axis_index("rad")
    radial_local = lax.dynamic_slice_in_dim(radial_factor, rad_index * rl, rl)
    damping_local = lax.dynamic_slice_in_dim(damping, rad_index * rl, rl)
    damp_full = damping_local[None, :, None, None]
    transform = angular_matrix(basis_first, basis_second, chan_table)
    vib_batched = jnp.broadcast_to(vib_coupling, (kl * rl, vc, vc))

    kinetic_batched = jnp.broadcast_to(kinetic_matrix, (kl, radial, radial))

    def to_radial_columns(x):
        blocks = jnp.transpose(x.reshape(kl, rl, n, mb), (2, 0, 1, 3))
        got = lax.all_to_all(blocks, "rad", 0, 0, tiled=True).reshape(n, kl, rl, mb)
        return jnp.transpose(got, (1, 0, 2, 3)).reshape(kl, radial, mb)

    def to_radial_rows(y):
        blocks = jnp.transpose(y.reshape(kl, n, rl, mb), (1, 0, 2, 3))
        got = lax.all_to_all(blocks, "rad", 0, 0, tiled=True).reshape(n, kl, rl, mb)
        return jnp.transpose(got, (1, 2, 0, 3)).reshape(kl, rl, vc, cc)

    def kinetic(columns):
        return jnp.einsum(
            "krs,ksm->krm",
            kinetic_batched,
            columns,
            precision=PRECISE,
            preferred_element_type=jnp.float32,
        )

    def local_part(current):
        angles = jnp.dot(
            current.reshape(-1, cc), transform.T, precision=PRECISE,
            preferred_element_type=jnp.float32,
        )
        angles = jnp.einsum(
            "buv,bva->bua",
            vib_batched,
            angles.reshape(kl * rl, vc, -1),
            precision=PRECISE,
            preferred_element_type=jnp.float32,
        )
        angles = angles.reshape(kl, rl, vc, -1) * potential[None, :, None, :]
        angular = jnp.dot(
            angles.reshape(-1, angles.shape[3]),
            transform,
            precision=PRECISE,
            preferred_element_type=jnp.float32,
        )
        weighted = coriolis[:, None, None, :] * current
        from_above = shifted(current[:1], "hel", -1)
        from_below = shifted(weighted[-1:], "hel", 1)
        upper_side = jnp.concatenate([current[1:], from_above], axis=0)
        lower_side = jnp.concatenate([from_below, weighted[:-1]], axis=0)
        return (
            angular.reshape(current.shape) + vib_energy[None, None, :, None] * current
        ) + radial_local[None, :, None, None] * (
            coriolis[:, None, None, :] * upper_side + lower_side
        )

    damp_columns = damping[None, :, None]
    earlier = prev_vector
    current = curr_vector
    columns = to_radial_columns(current)
    for iteration in range(STEPS - 1):
        rest = damp_full * (2.0 * local_part(current) - damp_full * earlier)
        following_columns = damp_columns * (2.0 * kinetic(columns)) + to_radial_columns(rest)
        earlier = current
        current = to_radial_rows(following_columns)
        columns = following_columns
    kinetic_image = to_radial_rows(kinetic(columns))
    image = kinetic_image + local_part(current)
    current = damp_full * (2.0 * image - damp_full * earlier)

    hel_index = lax.axis_index("hel")
    interp = interp_matrix(stencil, interp_weights, radial)
    qq = interp.shape[0]
    qb = qq // nh
    turn = jnp.arange(nh, dtype=jnp.int32)
    q_rows = (lax.rem(hel_index + turn, nh)[:, None] * qb + jnp.arange(qb)[None, :]).reshape(-1)
    interp_turned = jnp.broadcast_to(interp[q_rows], (kl, qq, radial))
    k_cols = (lax.rem(hel_index - turn + nh, nh)[:, None] * kl + jnp.arange(kl)[None, :]).reshape(-1)
    j_rows = (lax.rem(hel_index + turn, nh)[:, None] * kl + jnp.arange(kl)[None, :]).reshape(-1)
    frame_turned = frame_rotation[j_rows][:, k_cols]

    def hel_shift(x, d):
        if d == 0:
            return x
        return lax.ppermute(x, "hel", [(i, (i + d) % nh) for i in range(nh)])

    vchunks = 4 if vc % 4 == 0 else 1
    vs = vc // vchunks
    width = vs * cb
    results = []
    def finish(placed):
        arrived = [hel_shift(placed[:, d * qb:(d + 1) * qb], d) for d in range(nh)]
        gathered = jnp.stack(arrived, axis=0)
        turned = jnp.dot(
            frame_turned,
            gathered.reshape(nh * kl, qb * width),
            precision=PRECISE,
            preferred_element_type=jnp.float32,
        ).reshape(nh, kl, qb, width)
        back = [hel_shift(turned[e], e) for e in range(nh)]
        blocks = []
        for block in range(nh):
            source = lax.rem(hel_index - block + nh, nh)
            pick = back[0]
            for e in range(1, nh):
                pick = jnp.where(source == e, back[e], pick)
            blocks.append(pick)
        rotated = jnp.concatenate(blocks, axis=1)
        results.append(rotated.reshape(kl, qq, vs, cb))

    pending = None
    for i in range(vchunks):
        part = current[:, :, i * vs:(i + 1) * vs, :]
        if pending is not None:
            pending, part = lax.optimization_barrier((pending, part))
            finish(pending)
        chans = jnp.transpose(part.reshape(kl, rl, vs, n, cb), (3, 0, 1, 2, 4))
        got = lax.all_to_all(chans.reshape(n, kl, rl, width), "rad", 0, 0, tiled=True)
        radial_block = jnp.transpose(got.reshape(n, kl, rl, width), (1, 0, 2, 3)).reshape(
            kl, radial, width
        )
        placed = jnp.einsum(
            "kqr,krm->kqm",
            interp_turned,
            radial_block,
            precision=PRECISE,
            preferred_element_type=jnp.float32,
        )
        pending = placed
    finish(pending)
    product_amp = jnp.concatenate(results, axis=2)
    return (current, product_amp)


def solution(mesh):
    in_specs = (
        P("hel", "rad", None, None),
        P("hel", "rad", None, None),
        P(),
        P(),
        P(),
        P(),
        P("rad", None),
        P(),
        P(),
        P("hel", None),
        P(),
        P(),
        P(),
        P(),
        P(),
    )
    out_specs = (P("hel", "rad", None, None), P("hel", None, None, "rad"))
    return jax.shard_map(shards, mesh=mesh, in_specs=in_specs, out_specs=out_specs, check_vma=False)
```

```python
import jax
import jax.numpy as jnp
from jax import lax
from jax.sharding import PartitionSpec as P

STEPS = 2
PRECISE = lax.Precision.HIGHEST


def shifted(block, axis, distance):
    devices = range(lax.axis_size(axis))
    route = [(i - distance, i) for i in devices if i - distance in devices]
    return lax.ppermute(block, axis, route)


def angular_matrix(basis_first, basis_second, chan_table):
    levels = basis_first.shape[1]
    level_grid = jnp.arange(levels, dtype=jnp.int32)
    first_hot = (chan_table[None, :] // levels == level_grid[:, None]).astype(jnp.float32)
    second_hot = (chan_table[None, :] % levels == level_grid[:, None]).astype(jnp.float32)
    first_part = jnp.dot(
        basis_first, first_hot, precision=PRECISE, preferred_element_type=jnp.float32
    )
    second_part = jnp.dot(
        basis_second, second_hot, precision=PRECISE, preferred_element_type=jnp.float32
    )
    return first_part * second_part


def interp_matrix(stencil, interp_weights, radial_count):
    offsets = jnp.arange(4, dtype=jnp.int32)
    points = jnp.arange(radial_count, dtype=jnp.int32)
    matches = (points[None, None, :] == (stencil[:, None] + offsets[None, :])[:, :, None]).astype(
        jnp.float32
    )
    return jnp.sum(matches * interp_weights[:, :, None], axis=1)


def shards(
    prev_vector,
    curr_vector,
    kinetic_matrix,
    basis_first,
    basis_second,
    chan_table,
    potential,
    vib_coupling,
    vib_energy,
    coriolis,
    radial_factor,
    damping,
    stencil,
    interp_weights,
    frame_rotation,
):
    kl, rl, vc, cc = curr_vector.shape
    n = lax.axis_size("rad")
    nh = lax.axis_size("hel")
    radial = rl * n
    mb = vc * cc // n
    cb = cc // n
    rad_index = lax.axis_index("rad")
    radial_local = lax.dynamic_slice_in_dim(radial_factor, rad_index * rl, rl)
    damping_local = lax.dynamic_slice_in_dim(damping, rad_index * rl, rl)
    damp_full = damping_local[None, :, None, None]
    transform = angular_matrix(basis_first, basis_second, chan_table)
    vib_batched = jnp.broadcast_to(vib_coupling, (kl * rl, vc, vc))

    kinetic_batched = jnp.broadcast_to(kinetic_matrix, (kl, radial, radial))

    def to_radial_columns(x):
        blocks = jnp.transpose(x.reshape(kl, rl, n, mb), (2, 0, 1, 3))
        got = lax.all_to_all(blocks, "rad", 0, 0, tiled=True).reshape(n, kl, rl, mb)
        return jnp.transpose(got, (1, 0, 2, 3)).reshape(kl, radial, mb)

    def to_radial_rows(y):
        blocks = jnp.transpose(y.reshape(kl, n, rl, mb), (1, 0, 2, 3))
        got = lax.all_to_all(blocks, "rad", 0, 0, tiled=True).reshape(n, kl, rl, mb)
        return jnp.transpose(got, (1, 2, 0, 3)).reshape(kl, rl, vc, cc)

    def kinetic(columns):
        return jnp.einsum(
            "krs,ksm->krm",
            kinetic_batched,
            columns,
            precision=PRECISE,
            preferred_element_type=jnp.float32,
        )

    def local_part(current):
        angles = jnp.dot(
            current.reshape(-1, cc), transform.T, precision=PRECISE,
            preferred_element_type=jnp.float32,
        )
        angles = jnp.einsum(
            "buv,bva->bua",
            vib_batched,
            angles.reshape(kl * rl, vc, -1),
            precision=PRECISE,
            preferred_element_type=jnp.float32,
        )
        angles = angles.reshape(kl, rl, vc, -1) * potential[None, :, None, :]
        angular = jnp.dot(
            angles.reshape(-1, angles.shape[3]),
            transform,
            precision=PRECISE,
            preferred_element_type=jnp.float32,
        )
        weighted = coriolis[:, None, None, :] * current
        from_above = shifted(current[:1], "hel", -1)
        from_below = shifted(weighted[-1:], "hel", 1)
        upper_side = jnp.concatenate([current[1:], from_above], axis=0)
        lower_side = jnp.concatenate([from_below, weighted[:-1]], axis=0)
        return (
            angular.reshape(current.shape) + vib_energy[None, None, :, None] * current
        ) + radial_local[None, :, None, None] * (
            coriolis[:, None, None, :] * upper_side + lower_side
        )

    damp_columns = damping[None, :, None]
    earlier = prev_vector
    current = curr_vector
    columns = to_radial_columns(current)
    for iteration in range(STEPS - 1):
        rest = damp_full * (2.0 * local_part(current) - damp_full * earlier)
        following_columns = damp_columns * (2.0 * kinetic(columns)) + to_radial_columns(rest)
        earlier = current
        current = to_radial_rows(following_columns)
        columns = following_columns
    kinetic_image = to_radial_rows(kinetic(columns))
    local_image = local_part(current)
    if vc % 8 == 0:
        sizes = [vc // 4] * 3 + [vc // 8] * 2
    else:
        sizes = [vc]
    bounds = [sum(sizes[:i]) for i in range(len(sizes) + 1)]
    final_parts = []
    for lo, hi in zip(bounds[:-1], bounds[1:]):
        image = kinetic_image[:, :, lo:hi] + local_image[:, :, lo:hi]
        final_parts.append(damp_full * (2.0 * image - damp_full * earlier[:, :, lo:hi]))
    current = jnp.concatenate(final_parts, axis=2)

    hel_index = lax.axis_index("hel")
    interp = interp_matrix(stencil, interp_weights, radial)
    qq = interp.shape[0]
    qb = qq // nh
    turn = jnp.arange(nh, dtype=jnp.int32)
    q_rows = (lax.rem(hel_index + turn, nh)[:, None] * qb + jnp.arange(qb)[None, :]).reshape(-1)
    interp_turned = jnp.broadcast_to(interp[q_rows], (kl, qq, radial))
    k_cols = (lax.rem(hel_index - turn + nh, nh)[:, None] * kl + jnp.arange(kl)[None, :]).reshape(-1)
    j_rows = (lax.rem(hel_index + turn, nh)[:, None] * kl + jnp.arange(kl)[None, :]).reshape(-1)
    frame_turned = frame_rotation[j_rows][:, k_cols]

    def hel_shift(x, d):
        if d == 0:
            return x
        return lax.ppermute(x, "hel", [(i, (i + d) % nh) for i in range(nh)])

    results = []

    def finish(placed):
        vs = placed.shape[2] // cb
        width = vs * cb
        arrived = [hel_shift(placed[:, d * qb:(d + 1) * qb], d) for d in range(nh)]
        gathered = jnp.stack(arrived, axis=0)
        turned = jnp.dot(
            frame_turned,
            gathered.reshape(nh * kl, qb * width),
            precision=PRECISE,
            preferred_element_type=jnp.float32,
        ).reshape(nh, kl, qb, width)
        back = [hel_shift(turned[e], e) for e in range(nh)]
        blocks = []
        for block in range(nh):
            source = lax.rem(hel_index - block + nh, nh)
            pick = back[0]
            for e in range(1, nh):
                pick = jnp.where(source == e, back[e], pick)
            blocks.append(pick)
        rotated = jnp.concatenate(blocks, axis=1)
        results.append(rotated.reshape(kl, qq, vs, cb))

    pending = None
    for part in final_parts:
        vs = part.shape[2]
        width = vs * cb
        if pending is not None:
            pending, part = lax.optimization_barrier((pending, part))
            finish(pending)
        chans = jnp.transpose(part.reshape(kl, rl, vs, n, cb), (3, 0, 1, 2, 4))
        got = lax.all_to_all(chans.reshape(n, kl, rl, width), "rad", 0, 0, tiled=True)
        radial_block = jnp.transpose(got.reshape(n, kl, rl, width), (1, 0, 2, 3)).reshape(
            kl, radial, width
        )
        placed = jnp.einsum(
            "kqr,krm->kqm",
            interp_turned,
            radial_block,
            precision=PRECISE,
            preferred_element_type=jnp.float32,
        )
        pending = placed
    finish(pending)
    product_amp = jnp.concatenate(results, axis=2)
    return (current, product_amp)


def solution(mesh):
    in_specs = (
        P("hel", "rad", None, None),
        P("hel", "rad", None, None),
        P(),
        P(),
        P(),
        P(),
        P("rad", None),
        P(),
        P(),
        P("hel", None),
        P(),
        P(),
        P(),
        P(),
        P(),
    )
    out_specs = (P("hel", "rad", None, None), P("hel", None, None, "rad"))
    return jax.shard_map(shards, mesh=mesh, in_specs=in_specs, out_specs=out_specs, check_vma=False)
```

```python
import jax
import jax.numpy as jnp
from jax import lax
from jax.sharding import PartitionSpec as P

STEPS = 2
PRECISE = lax.Precision.HIGHEST


def shifted(block, axis, distance):
    devices = range(lax.axis_size(axis))
    route = [(i - distance, i) for i in devices if i - distance in devices]
    return lax.ppermute(block, axis, route)


def angular_matrix(basis_first, basis_second, chan_table):
    levels = basis_first.shape[1]
    level_grid = jnp.arange(levels, dtype=jnp.int32)
    first_hot = (chan_table[None, :] // levels == level_grid[:, None]).astype(jnp.float32)
    second_hot = (chan_table[None, :] % levels == level_grid[:, None]).astype(jnp.float32)
    first_part = jnp.dot(
        basis_first, first_hot, precision=PRECISE, preferred_element_type=jnp.float32
    )
    second_part = jnp.dot(
        basis_second, second_hot, precision=PRECISE, preferred_element_type=jnp.float32
    )
    return first_part * second_part


def interp_matrix(stencil, interp_weights, radial_count):
    offsets = jnp.arange(4, dtype=jnp.int32)
    points = jnp.arange(radial_count, dtype=jnp.int32)
    matches = (points[None, None, :] == (stencil[:, None] + offsets[None, :])[:, :, None]).astype(
        jnp.float32
    )
    return jnp.sum(matches * interp_weights[:, :, None], axis=1)


def shards(
    prev_vector,
    curr_vector,
    kinetic_matrix,
    basis_first,
    basis_second,
    chan_table,
    potential,
    vib_coupling,
    vib_energy,
    coriolis,
    radial_factor,
    damping,
    stencil,
    interp_weights,
    frame_rotation,
):
    kl, rl, vc, cc = curr_vector.shape
    n = lax.axis_size("rad")
    nh = lax.axis_size("hel")
    radial = rl * n
    mb = vc * cc // n
    cb = cc // n
    rad_index = lax.axis_index("rad")
    radial_local = lax.dynamic_slice_in_dim(radial_factor, rad_index * rl, rl)
    damping_local = lax.dynamic_slice_in_dim(damping, rad_index * rl, rl)
    damp_full = damping_local[None, :, None, None]
    transform = angular_matrix(basis_first, basis_second, chan_table)
    vib_batched = jnp.broadcast_to(vib_coupling, (kl * rl, vc, vc))

    kinetic_batched = jnp.broadcast_to(kinetic_matrix, (kl, radial, radial))

    def to_radial_columns(x):
        blocks = jnp.transpose(x.reshape(kl, rl, n, mb), (2, 0, 1, 3))
        got = lax.all_to_all(blocks, "rad", 0, 0, tiled=True).reshape(n, kl, rl, mb)
        return jnp.transpose(got, (1, 0, 2, 3)).reshape(kl, radial, mb)

    def to_radial_rows(y, companion=None):
        blocks = jnp.transpose(y.reshape(kl, n, rl, mb), (1, 0, 2, 3))
        got = lax.all_to_all(blocks, "rad", 0, 0, tiled=True).reshape(n, kl, rl, mb)
        if companion is not None:
            companion, got = lax.optimization_barrier((companion, got))
        return jnp.transpose(got, (1, 2, 0, 3)).reshape(kl, rl, vc, cc), companion

    def kinetic(columns):
        return jnp.einsum(
            "krs,ksm->krm",
            kinetic_batched,
            columns,
            precision=PRECISE,
            preferred_element_type=jnp.float32,
        )

    def local_part(current):
        angles = jnp.dot(
            current.reshape(-1, cc), transform.T, precision=PRECISE,
            preferred_element_type=jnp.float32,
        )
        angles = jnp.einsum(
            "buv,bva->bua",
            vib_batched,
            angles.reshape(kl * rl, vc, -1),
            precision=PRECISE,
            preferred_element_type=jnp.float32,
        )
        angles = angles.reshape(kl, rl, vc, -1) * potential[None, :, None, :]
        angular = jnp.dot(
            angles.reshape(-1, angles.shape[3]),
            transform,
            precision=PRECISE,
            preferred_element_type=jnp.float32,
        )
        weighted = coriolis[:, None, None, :] * current
        from_above = shifted(current[:1], "hel", -1)
        from_below = shifted(weighted[-1:], "hel", 1)
        upper_side = jnp.concatenate([current[1:], from_above], axis=0)
        lower_side = jnp.concatenate([from_below, weighted[:-1]], axis=0)
        return (
            angular.reshape(current.shape) + vib_energy[None, None, :, None] * current
        ) + radial_local[None, :, None, None] * (
            coriolis[:, None, None, :] * upper_side + lower_side
        )

    damp_columns = damping[None, :, None]
    earlier = prev_vector
    current = curr_vector
    columns = to_radial_columns(current)
    for iteration in range(STEPS - 1):
        rest = damp_full * (2.0 * local_part(current) - damp_full * earlier)
        following_columns = damp_columns * (2.0 * kinetic(columns)) + to_radial_columns(rest)
        earlier = current
        current, _ = to_radial_rows(following_columns)
        columns = following_columns
    kinetic_image, local_image = to_radial_rows(kinetic(columns), local_part(current))
    image = kinetic_image + local_image
    current = damp_full * (2.0 * image - damp_full * earlier)

    hel_index = lax.axis_index("hel")
    interp = interp_matrix(stencil, interp_weights, radial)
    qq = interp.shape[0]
    qb = qq // nh
    turn = jnp.arange(nh, dtype=jnp.int32)
    q_rows = (lax.rem(hel_index + turn, nh)[:, None] * qb + jnp.arange(qb)[None, :]).reshape(-1)
    interp_turned = jnp.broadcast_to(interp[q_rows], (kl, qq, radial))
    k_cols = (lax.rem(hel_index - turn + nh, nh)[:, None] * kl + jnp.arange(kl)[None, :]).reshape(-1)
    j_rows = (lax.rem(hel_index + turn, nh)[:, None] * kl + jnp.arange(kl)[None, :]).reshape(-1)
    frame_turned = frame_rotation[j_rows][:, k_cols]

    def hel_shift(x, d):
        if d == 0:
            return x
        return lax.ppermute(x, "hel", [(i, (i + d) % nh) for i in range(nh)])

    vchunks = 4 if vc % 4 == 0 else 1
    vs = vc // vchunks
    width = vs * cb
    results = []
    def finish(placed):
        arrived = [hel_shift(placed[:, d * qb:(d + 1) * qb], d) for d in range(nh)]
        gathered = jnp.stack(arrived, axis=0)
        turned = jnp.dot(
            frame_turned,
            gathered.reshape(nh * kl, qb * width),
            precision=PRECISE,
            preferred_element_type=jnp.float32,
        ).reshape(nh, kl, qb, width)
        back = [hel_shift(turned[e], e) for e in range(nh)]
        blocks = []
        for block in range(nh):
            source = lax.rem(hel_index - block + nh, nh)
            pick = back[0]
            for e in range(1, nh):
                pick = jnp.where(source == e, back[e], pick)
            blocks.append(pick)
        rotated = jnp.concatenate(blocks, axis=1)
        results.append(rotated.reshape(kl, qq, vs, cb))

    pending = None
    for i in range(vchunks):
        part = current[:, :, i * vs:(i + 1) * vs, :]
        if pending is not None:
            pending, part = lax.optimization_barrier((pending, part))
            finish(pending)
        chans = jnp.transpose(part.reshape(kl, rl, vs, n, cb), (3, 0, 1, 2, 4))
        got = lax.all_to_all(chans.reshape(n, kl, rl, width), "rad", 0, 0, tiled=True)
        radial_block = jnp.transpose(got.reshape(n, kl, rl, width), (1, 0, 2, 3)).reshape(
            kl, radial, width
        )
        placed = jnp.einsum(
            "kqr,krm->kqm",
            interp_turned,
            radial_block,
            precision=PRECISE,
            preferred_element_type=jnp.float32,
        )
        pending = placed
    finish(pending)
    product_amp = jnp.concatenate(results, axis=2)
    return (current, product_amp)


def solution(mesh):
    in_specs = (
        P("hel", "rad", None, None),
        P("hel", "rad", None, None),
        P(),
        P(),
        P(),
        P(),
        P("rad", None),
        P(),
        P(),
        P("hel", None),
        P(),
        P(),
        P(),
        P(),
        P(),
    )
    out_specs = (P("hel", "rad", None, None), P("hel", None, None, "rad"))
    return jax.shard_map(shards, mesh=mesh, in_specs=in_specs, out_specs=out_specs, check_vma=False)
```

```python
import jax
import jax.numpy as jnp
from jax import lax
from jax.sharding import PartitionSpec as P

STEPS = 2
PRECISE = lax.Precision.HIGHEST


def shifted(block, axis, distance):
    devices = range(lax.axis_size(axis))
    route = [(i - distance, i) for i in devices if i - distance in devices]
    return lax.ppermute(block, axis, route)


def angular_matrix(basis_first, basis_second, chan_table):
    levels = basis_first.shape[1]
    level_grid = jnp.arange(levels, dtype=jnp.int32)
    first_hot = (chan_table[None, :] // levels == level_grid[:, None]).astype(jnp.float32)
    second_hot = (chan_table[None, :] % levels == level_grid[:, None]).astype(jnp.float32)
    first_part = jnp.dot(
        basis_first, first_hot, precision=PRECISE, preferred_element_type=jnp.float32
    )
    second_part = jnp.dot(
        basis_second, second_hot, precision=PRECISE, preferred_element_type=jnp.float32
    )
    return first_part * second_part


def interp_matrix(stencil, interp_weights, radial_count):
    offsets = jnp.arange(4, dtype=jnp.int32)
    points = jnp.arange(radial_count, dtype=jnp.int32)
    matches = (points[None, None, :] == (stencil[:, None] + offsets[None, :])[:, :, None]).astype(
        jnp.float32
    )
    return jnp.sum(matches * interp_weights[:, :, None], axis=1)


def shards(
    prev_vector,
    curr_vector,
    kinetic_matrix,
    basis_first,
    basis_second,
    chan_table,
    potential,
    vib_coupling,
    vib_energy,
    coriolis,
    radial_factor,
    damping,
    stencil,
    interp_weights,
    frame_rotation,
):
    kl, rl, vc, cc = curr_vector.shape
    n = lax.axis_size("rad")
    nh = lax.axis_size("hel")
    radial = rl * n
    mb = vc * cc // n
    cb = cc // n
    rad_index = lax.axis_index("rad")
    radial_local = lax.dynamic_slice_in_dim(radial_factor, rad_index * rl, rl)
    damping_local = lax.dynamic_slice_in_dim(damping, rad_index * rl, rl)
    damp_full = damping_local[None, :, None, None]
    transform = angular_matrix(basis_first, basis_second, chan_table)
    vib_batched = jnp.broadcast_to(vib_coupling, (kl * rl, vc, vc))

    kinetic_batched = jnp.broadcast_to(kinetic_matrix, (kl, radial, radial))

    def to_radial_columns(x):
        blocks = jnp.transpose(x.reshape(kl, rl, n, mb), (2, 0, 1, 3))
        got = lax.all_to_all(blocks, "rad", 0, 0, tiled=True).reshape(n, kl, rl, mb)
        return jnp.transpose(got, (1, 0, 2, 3)).reshape(kl, radial, mb)

    def to_radial_rows(y, companion=None):
        blocks = jnp.transpose(y.reshape(kl, n, rl, mb), (1, 0, 2, 3))
        got = lax.all_to_all(blocks, "rad", 0, 0, tiled=True).reshape(n, kl, rl, mb)
        if companion is not None:
            companion, got = lax.optimization_barrier((companion, got))
        return jnp.transpose(got, (1, 2, 0, 3)).reshape(kl, rl, vc, cc), companion

    def kinetic(columns):
        return jnp.einsum(
            "krs,ksm->krm",
            kinetic_batched,
            columns,
            precision=PRECISE,
            preferred_element_type=jnp.float32,
        )

    def local_part(current):
        angles = jnp.dot(
            current.reshape(-1, cc), transform.T, precision=PRECISE,
            preferred_element_type=jnp.float32,
        )
        angles = jnp.einsum(
            "buv,bva->bua",
            vib_batched,
            angles.reshape(kl * rl, vc, -1),
            precision=PRECISE,
            preferred_element_type=jnp.float32,
        )
        angles = angles.reshape(kl, rl, vc, -1) * potential[None, :, None, :]
        angular = jnp.dot(
            angles.reshape(-1, angles.shape[3]),
            transform,
            precision=PRECISE,
            preferred_element_type=jnp.float32,
        )
        weighted = coriolis[:, None, None, :] * current
        from_above = shifted(current[:1], "hel", -1)
        from_below = shifted(weighted[-1:], "hel", 1)
        upper_side = jnp.concatenate([current[1:], from_above], axis=0)
        lower_side = jnp.concatenate([from_below, weighted[:-1]], axis=0)
        return (
            angular.reshape(current.shape) + vib_energy[None, None, :, None] * current
        ) + radial_local[None, :, None, None] * (
            coriolis[:, None, None, :] * upper_side + lower_side
        )

    damp_columns = damping[None, :, None]
    earlier = prev_vector
    current = curr_vector
    columns = to_radial_columns(current)
    for iteration in range(STEPS - 1):
        rest = damp_full * (2.0 * local_part(current) - damp_full * earlier)
        following_columns = damp_columns * (2.0 * kinetic(columns)) + to_radial_columns(rest)
        earlier = current
        current, _ = to_radial_rows(following_columns)
        columns = following_columns
    kinetic_image, local_image = to_radial_rows(kinetic(columns), local_part(current))
    image = kinetic_image + local_image
    current = damp_full * (2.0 * image - damp_full * earlier)

    interp = interp_matrix(stencil, interp_weights, radial)
    qq = interp.shape[0]
    vb = vc // nh
    split_v = jnp.transpose(current.reshape(kl, rl, nh, vb, cc), (2, 0, 1, 3, 4))
    all_k = lax.all_to_all(split_v, "hel", 0, 0, tiled=True)
    turned = jnp.dot(
        frame_rotation,
        all_k.reshape(nh * kl, rl * vb * cc),
        precision=PRECISE,
        preferred_element_type=jnp.float32,
    )
    outgoing = jnp.transpose(turned.reshape(nh, kl, rl, vb, n, cb), (0, 4, 1, 2, 3, 5))
    arrived = lax.all_to_all(
        outgoing.reshape(nh * n, kl, rl, vb * cb), ("hel", "rad"), 0, 0, tiled=True
    )
    columns = jnp.transpose(arrived.reshape(nh, n, kl, rl, vb, cb), (2, 1, 3, 0, 4, 5))
    product_amp = jnp.einsum(
        "kqr,krm->kqm",
        jnp.broadcast_to(interp, (kl, qq, radial)),
        columns.reshape(kl, radial, vc * cb),
        precision=PRECISE,
        preferred_element_type=jnp.float32,
    ).reshape(kl, qq, vc, cb)
    return (current, product_amp)


def solution(mesh):
    in_specs = (
        P("hel", "rad", None, None),
        P("hel", "rad", None, None),
        P(),
        P(),
        P(),
        P(),
        P("rad", None),
        P(),
        P(),
        P("hel", None),
        P(),
        P(),
        P(),
        P(),
        P(),
    )
    out_specs = (P("hel", "rad", None, None), P("hel", None, None, "rad"))
    return jax.shard_map(shards, mesh=mesh, in_specs=in_specs, out_specs=out_specs, check_vma=False)
```

```python
import jax
import jax.numpy as jnp
from jax import lax
from jax.sharding import PartitionSpec as P

STEPS = 2
PRECISE = lax.Precision.HIGHEST


def shifted(block, axis, distance):
    devices = range(lax.axis_size(axis))
    route = [(i - distance, i) for i in devices if i - distance in devices]
    return lax.ppermute(block, axis, route)


def angular_matrix(basis_first, basis_second, chan_table):
    levels = basis_first.shape[1]
    level_grid = jnp.arange(levels, dtype=jnp.int32)
    first_hot = (chan_table[None, :] // levels == level_grid[:, None]).astype(jnp.float32)
    second_hot = (chan_table[None, :] % levels == level_grid[:, None]).astype(jnp.float32)
    first_part = jnp.dot(
        basis_first, first_hot, precision=PRECISE, preferred_element_type=jnp.float32
    )
    second_part = jnp.dot(
        basis_second, second_hot, precision=PRECISE, preferred_element_type=jnp.float32
    )
    return first_part * second_part


def interp_matrix(stencil, interp_weights, radial_count):
    offsets = jnp.arange(4, dtype=jnp.int32)
    points = jnp.arange(radial_count, dtype=jnp.int32)
    matches = (points[None, None, :] == (stencil[:, None] + offsets[None, :])[:, :, None]).astype(
        jnp.float32
    )
    return jnp.sum(matches * interp_weights[:, :, None], axis=1)


def shards(
    prev_vector,
    curr_vector,
    kinetic_matrix,
    basis_first,
    basis_second,
    chan_table,
    potential,
    vib_coupling,
    vib_energy,
    coriolis,
    radial_factor,
    damping,
    stencil,
    interp_weights,
    frame_rotation,
):
    kl, rl, vc, cc = curr_vector.shape
    n = lax.axis_size("rad")
    nh = lax.axis_size("hel")
    radial = rl * n
    mb = vc * cc // n
    cb = cc // n
    rad_index = lax.axis_index("rad")
    radial_local = lax.dynamic_slice_in_dim(radial_factor, rad_index * rl, rl)
    damping_local = lax.dynamic_slice_in_dim(damping, rad_index * rl, rl)
    damp_full = damping_local[None, :, None, None]
    transform = angular_matrix(basis_first, basis_second, chan_table)
    vib_batched = jnp.broadcast_to(vib_coupling, (kl * rl, vc, vc))

    kinetic_batched = jnp.broadcast_to(kinetic_matrix, (kl, radial, radial))

    def to_radial_columns(x):
        blocks = jnp.transpose(x.reshape(kl, rl, n, mb), (2, 0, 1, 3))
        got = lax.all_to_all(blocks, "rad", 0, 0, tiled=True).reshape(n, kl, rl, mb)
        return jnp.transpose(got, (1, 0, 2, 3)).reshape(kl, radial, mb)

    def to_radial_rows(y, companion=None):
        blocks = jnp.transpose(y.reshape(kl, n, rl, mb), (1, 0, 2, 3))
        got = lax.all_to_all(blocks, "rad", 0, 0, tiled=True).reshape(n, kl, rl, mb)
        if companion is not None:
            companion, got = lax.optimization_barrier((companion, got))
        return jnp.transpose(got, (1, 2, 0, 3)).reshape(kl, rl, vc, cc), companion

    def kinetic(columns):
        return jnp.einsum(
            "krs,ksm->krm",
            kinetic_batched,
            columns,
            precision=PRECISE,
            preferred_element_type=jnp.float32,
        )

    def local_part(current):
        angles = jnp.dot(
            current.reshape(-1, cc), transform.T, precision=PRECISE,
            preferred_element_type=jnp.float32,
        )
        angles = jnp.einsum(
            "buv,bva->bua",
            vib_batched,
            angles.reshape(kl * rl, vc, -1),
            precision=PRECISE,
            preferred_element_type=jnp.float32,
        )
        angles = angles.reshape(kl, rl, vc, -1) * potential[None, :, None, :]
        angular = jnp.dot(
            angles.reshape(-1, angles.shape[3]),
            transform,
            precision=PRECISE,
            preferred_element_type=jnp.float32,
        )
        weighted = coriolis[:, None, None, :] * current
        from_above = shifted(current[:1], "hel", -1)
        from_below = shifted(weighted[-1:], "hel", 1)
        upper_side = jnp.concatenate([current[1:], from_above], axis=0)
        lower_side = jnp.concatenate([from_below, weighted[:-1]], axis=0)
        return (
            angular.reshape(current.shape) + vib_energy[None, None, :, None] * current
        ) + radial_local[None, :, None, None] * (
            coriolis[:, None, None, :] * upper_side + lower_side
        )

    damp_columns = damping[None, :, None]
    earlier = prev_vector
    current = curr_vector
    columns = to_radial_columns(current)
    for iteration in range(STEPS - 1):
        rest = damp_full * (2.0 * local_part(current) - damp_full * earlier)
        following_columns = damp_columns * (2.0 * kinetic(columns)) + to_radial_columns(rest)
        earlier = current
        current, _ = to_radial_rows(following_columns)
        columns = following_columns
    kinetic_image, local_image = to_radial_rows(kinetic(columns), local_part(current))
    image = kinetic_image + local_image
    current = damp_full * (2.0 * image - damp_full * earlier)

    hel_index = lax.axis_index("hel")
    interp = interp_matrix(stencil, interp_weights, radial)
    qq = interp.shape[0]
    qb = qq // nh
    turn = jnp.arange(nh, dtype=jnp.int32)
    q_rows = (lax.rem(hel_index + turn, nh)[:, None] * qb + jnp.arange(qb)[None, :]).reshape(-1)
    interp_turned = jnp.broadcast_to(interp[q_rows], (kl, qq, radial))
    k_cols = (lax.rem(hel_index - turn + nh, nh)[:, None] * kl + jnp.arange(kl)[None, :]).reshape(-1)
    j_rows = (lax.rem(hel_index + turn, nh)[:, None] * kl + jnp.arange(kl)[None, :]).reshape(-1)
    frame_turned = frame_rotation[j_rows][:, k_cols]

    def hel_shift(x, d):
        if d == 0:
            return x
        return lax.ppermute(x, "hel", [(i, (i + d) % nh) for i in range(nh)])

    if vc % 8 == 0:
        sizes = [vc // 8] + [vc // 4] * 3 + [vc // 8]
    else:
        sizes = [vc]
    bounds = [sum(sizes[:i]) for i in range(len(sizes) + 1)]
    results = []

    def finish(placed):
        vs = placed.shape[2] // cb
        width = vs * cb
        arrived = [hel_shift(placed[:, d * qb:(d + 1) * qb], d) for d in range(nh)]
        gathered = jnp.stack(arrived, axis=0)
        turned = jnp.dot(
            frame_turned,
            gathered.reshape(nh * kl, qb * width),
            precision=PRECISE,
            preferred_element_type=jnp.float32,
        ).reshape(nh, kl, qb, width)
        back = [hel_shift(turned[e], e) for e in range(nh)]
        blocks = []
        for block in range(nh):
            source = lax.rem(hel_index - block + nh, nh)
            pick = back[0]
            for e in range(1, nh):
                pick = jnp.where(source == e, back[e], pick)
            blocks.append(pick)
        rotated = jnp.concatenate(blocks, axis=1)
        results.append(rotated.reshape(kl, qq, vs, cb))

    pending = None
    for lo, hi in zip(bounds[:-1], bounds[1:]):
        part = current[:, :, lo:hi, :]
        vs = hi - lo
        width = vs * cb
        if pending is not None:
            pending, part = lax.optimization_barrier((pending, part))
            finish(pending)
        chans = jnp.transpose(part.reshape(kl, rl, vs, n, cb), (3, 0, 1, 2, 4))
        got = lax.all_to_all(chans.reshape(n, kl, rl, width), "rad", 0, 0, tiled=True)
        radial_block = jnp.transpose(got.reshape(n, kl, rl, width), (1, 0, 2, 3)).reshape(
            kl, radial, width
        )
        placed = jnp.einsum(
            "kqr,krm->kqm",
            interp_turned,
            radial_block,
            precision=PRECISE,
            preferred_element_type=jnp.float32,
        )
        pending = placed
    finish(pending)
    product_amp = jnp.concatenate(results, axis=2)
    return (current, product_amp)


def solution(mesh):
    in_specs = (
        P("hel", "rad", None, None),
        P("hel", "rad", None, None),
        P(),
        P(),
        P(),
        P(),
        P("rad", None),
        P(),
        P(),
        P("hel", None),
        P(),
        P(),
        P(),
        P(),
        P(),
    )
    out_specs = (P("hel", "rad", None, None), P("hel", None, None, "rad"))
    return jax.shard_map(shards, mesh=mesh, in_specs=in_specs, out_specs=out_specs, check_vma=False)
```

```python
import jax
import jax.numpy as jnp
from jax import lax
from jax.sharding import PartitionSpec as P

STEPS = 2
PRECISE = lax.Precision.HIGHEST


def shifted(block, axis, distance):
    devices = range(lax.axis_size(axis))
    route = [(i - distance, i) for i in devices if i - distance in devices]
    return lax.ppermute(block, axis, route)


def angular_matrix(basis_first, basis_second, chan_table):
    levels = basis_first.shape[1]
    level_grid = jnp.arange(levels, dtype=jnp.int32)
    first_hot = (chan_table[None, :] // levels == level_grid[:, None]).astype(jnp.float32)
    second_hot = (chan_table[None, :] % levels == level_grid[:, None]).astype(jnp.float32)
    first_part = jnp.dot(
        basis_first, first_hot, precision=PRECISE, preferred_element_type=jnp.float32
    )
    second_part = jnp.dot(
        basis_second, second_hot, precision=PRECISE, preferred_element_type=jnp.float32
    )
    return first_part * second_part


def interp_matrix(stencil, interp_weights, radial_count):
    offsets = jnp.arange(4, dtype=jnp.int32)
    points = jnp.arange(radial_count, dtype=jnp.int32)
    matches = (points[None, None, :] == (stencil[:, None] + offsets[None, :])[:, :, None]).astype(
        jnp.float32
    )
    return jnp.sum(matches * interp_weights[:, :, None], axis=1)


def shards(
    prev_vector,
    curr_vector,
    kinetic_matrix,
    basis_first,
    basis_second,
    chan_table,
    potential,
    vib_coupling,
    vib_energy,
    coriolis,
    radial_factor,
    damping,
    stencil,
    interp_weights,
    frame_rotation,
):
    kl, rl, vc, cc = curr_vector.shape
    n = lax.axis_size("rad")
    nh = lax.axis_size("hel")
    radial = rl * n
    mb = vc * cc // n
    cb = cc // n
    rad_index = lax.axis_index("rad")
    radial_local = lax.dynamic_slice_in_dim(radial_factor, rad_index * rl, rl)
    damping_local = lax.dynamic_slice_in_dim(damping, rad_index * rl, rl)
    damp_full = damping_local[None, :, None, None]
    transform = angular_matrix(basis_first, basis_second, chan_table)
    vib_batched = jnp.broadcast_to(vib_coupling, (kl * rl, vc, vc))

    kinetic_batched = jnp.broadcast_to(kinetic_matrix, (kl, radial, radial))

    def to_radial_columns(x):
        blocks = jnp.transpose(x.reshape(kl, rl, n, mb), (2, 0, 1, 3))
        got = lax.all_to_all(blocks, "rad", 0, 0, tiled=True).reshape(n, kl, rl, mb)
        return jnp.transpose(got, (1, 0, 2, 3)).reshape(kl, radial, mb)

    def to_radial_rows(y, companion=None):
        blocks = jnp.transpose(y.reshape(kl, n, rl, mb), (1, 0, 2, 3))
        got = lax.all_to_all(blocks, "rad", 0, 0, tiled=True).reshape(n, kl, rl, mb)
        if companion is not None:
            companion, got = lax.optimization_barrier((companion, got))
        return jnp.transpose(got, (1, 2, 0, 3)).reshape(kl, rl, vc, cc), companion

    def kinetic(columns):
        return jnp.einsum(
            "krs,ksm->krm",
            kinetic_batched,
            columns,
            precision=PRECISE,
            preferred_element_type=jnp.float32,
        )

    def local_part(current):
        angles = jnp.dot(
            current.reshape(-1, cc), transform.T, precision=PRECISE,
            preferred_element_type=jnp.float32,
        )
        angles = jnp.einsum(
            "buv,bva->bua",
            vib_batched,
            angles.reshape(kl * rl, vc, -1),
            precision=PRECISE,
            preferred_element_type=jnp.float32,
        )
        angles = angles.reshape(kl, rl, vc, -1) * potential[None, :, None, :]
        angular = jnp.dot(
            angles.reshape(-1, angles.shape[3]),
            transform,
            precision=PRECISE,
            preferred_element_type=jnp.float32,
        )
        weighted = coriolis[:, None, None, :] * current
        from_above = shifted(current[:1], "hel", -1)
        from_below = shifted(weighted[-1:], "hel", 1)
        upper_side = jnp.concatenate([current[1:], from_above], axis=0)
        lower_side = jnp.concatenate([from_below, weighted[:-1]], axis=0)
        return (
            angular.reshape(current.shape) + vib_energy[None, None, :, None] * current
        ) + radial_local[None, :, None, None] * (
            coriolis[:, None, None, :] * upper_side + lower_side
        )

    damp_columns = damping[None, :, None]
    earlier = prev_vector
    current = curr_vector
    columns = to_radial_columns(current)
    for iteration in range(STEPS - 1):
        rest = damp_full * (2.0 * local_part(current) - damp_full * earlier)
        following_columns = damp_columns * (2.0 * kinetic(columns)) + to_radial_columns(rest)
        earlier = current
        current, _ = to_radial_rows(following_columns)
        columns = following_columns
    kinetic_image, local_image = to_radial_rows(kinetic(columns), local_part(current))
    image = kinetic_image + local_image
    current = damp_full * (2.0 * image - damp_full * earlier)

    hel_index = lax.axis_index("hel")
    interp = interp_matrix(stencil, interp_weights, radial)
    qq = interp.shape[0]
    qb = qq // nh
    turn = jnp.arange(nh, dtype=jnp.int32)
    q_rows = (lax.rem(hel_index + turn, nh)[:, None] * qb + jnp.arange(qb)[None, :]).reshape(-1)
    interp_turned = jnp.broadcast_to(interp[q_rows], (kl, qq, radial))
    k_cols = (lax.rem(hel_index - turn + nh, nh)[:, None] * kl + jnp.arange(kl)[None, :]).reshape(-1)
    j_rows = (lax.rem(hel_index + turn, nh)[:, None] * kl + jnp.arange(kl)[None, :]).reshape(-1)
    frame_turned = frame_rotation[j_rows][:, k_cols]
    rad_turn = jnp.arange(n, dtype=jnp.int32)
    r_cols = (lax.rem(rad_index - rad_turn + n, n)[:, None] * rl + jnp.arange(rl)[None, :]).reshape(-1)
    interp_turned = interp_turned[:, :, r_cols]

    def rad_shift(x, d):
        if d == 0:
            return x
        return lax.ppermute(x, "rad", [(i, (i + d) % n) for i in range(n)])

    def hel_shift(x, d):
        if d == 0:
            return x
        return lax.ppermute(x, "hel", [(i, (i + d) % nh) for i in range(nh)])

    if vc % 8 == 0:
        sizes = [vc // 8] + [vc // 4] * 3 + [vc // 8]
    else:
        sizes = [vc]
    bounds = [sum(sizes[:i]) for i in range(len(sizes) + 1)]
    results = []

    def finish(placed):
        vs = placed.shape[2] // cb
        width = vs * cb
        arrived = [hel_shift(placed[:, d * qb:(d + 1) * qb], d) for d in range(nh)]
        gathered = jnp.stack(arrived, axis=0)
        turned = jnp.dot(
            frame_turned,
            gathered.reshape(nh * kl, qb * width),
            precision=PRECISE,
            preferred_element_type=jnp.float32,
        ).reshape(nh, kl, qb, width)
        back = [hel_shift(turned[e], e) for e in range(nh)]
        blocks = []
        for block in range(nh):
            source = lax.rem(hel_index - block + nh, nh)
            pick = back[0]
            for e in range(1, nh):
                pick = jnp.where(source == e, back[e], pick)
            blocks.append(pick)
        rotated = jnp.concatenate(blocks, axis=1)
        results.append(rotated.reshape(kl, qq, vs, cb))

    pending = None
    for lo, hi in zip(bounds[:-1], bounds[1:]):
        part = current[:, :, lo:hi, :]
        vs = hi - lo
        width = vs * cb
        if pending is not None:
            pending, part = lax.optimization_barrier((pending, part))
            finish(pending)
        chans = jnp.transpose(part.reshape(kl, rl, vs, n, cb), (3, 0, 1, 2, 4))
        chans = chans.reshape(n, kl, rl, width)
        rolled = lax.dynamic_slice_in_dim(
            jnp.concatenate([chans, chans], axis=0), rad_index, n, axis=0
        )
        got = jnp.stack([rad_shift(rolled[d], d) for d in range(n)], axis=0)
        radial_block = jnp.transpose(got, (1, 0, 2, 3)).reshape(kl, radial, width)
        placed = jnp.einsum(
            "kqr,krm->kqm",
            interp_turned,
            radial_block,
            precision=PRECISE,
            preferred_element_type=jnp.float32,
        )
        pending = placed
    finish(pending)
    product_amp = jnp.concatenate(results, axis=2)
    return (current, product_amp)


def solution(mesh):
    in_specs = (
        P("hel", "rad", None, None),
        P("hel", "rad", None, None),
        P(),
        P(),
        P(),
        P(),
        P("rad", None),
        P(),
        P(),
        P("hel", None),
        P(),
        P(),
        P(),
        P(),
        P(),
    )
    out_specs = (P("hel", "rad", None, None), P("hel", None, None, "rad"))
    return jax.shard_map(shards, mesh=mesh, in_specs=in_specs, out_specs=out_specs, check_vma=False)
```

```python
import jax
import jax.numpy as jnp
from jax import lax
from jax.sharding import PartitionSpec as P

STEPS = 2
PRECISE = lax.Precision.HIGHEST


def shifted(block, axis, distance):
    devices = range(lax.axis_size(axis))
    route = [(i - distance, i) for i in devices if i - distance in devices]
    return lax.ppermute(block, axis, route)


def angular_matrix(basis_first, basis_second, chan_table):
    levels = basis_first.shape[1]
    level_grid = jnp.arange(levels, dtype=jnp.int32)
    first_hot = (chan_table[None, :] // levels == level_grid[:, None]).astype(jnp.float32)
    second_hot = (chan_table[None, :] % levels == level_grid[:, None]).astype(jnp.float32)
    first_part = jnp.dot(
        basis_first, first_hot, precision=PRECISE, preferred_element_type=jnp.float32
    )
    second_part = jnp.dot(
        basis_second, second_hot, precision=PRECISE, preferred_element_type=jnp.float32
    )
    return first_part * second_part


def interp_matrix(stencil, interp_weights, radial_count):
    offsets = jnp.arange(4, dtype=jnp.int32)
    points = jnp.arange(radial_count, dtype=jnp.int32)
    matches = (points[None, None, :] == (stencil[:, None] + offsets[None, :])[:, :, None]).astype(
        jnp.float32
    )
    return jnp.sum(matches * interp_weights[:, :, None], axis=1)


def shards(
    prev_vector,
    curr_vector,
    kinetic_matrix,
    basis_first,
    basis_second,
    chan_table,
    potential,
    vib_coupling,
    vib_energy,
    coriolis,
    radial_factor,
    damping,
    stencil,
    interp_weights,
    frame_rotation,
):
    kl, rl, vc, cc = curr_vector.shape
    n = lax.axis_size("rad")
    nh = lax.axis_size("hel")
    radial = rl * n
    mb = vc * cc // n
    cb = cc // n
    rad_index = lax.axis_index("rad")
    radial_local = lax.dynamic_slice_in_dim(radial_factor, rad_index * rl, rl)
    damping_local = lax.dynamic_slice_in_dim(damping, rad_index * rl, rl)
    damp_full = damping_local[None, :, None, None]
    transform = angular_matrix(basis_first, basis_second, chan_table)
    vib_batched = jnp.broadcast_to(vib_coupling, (kl * rl, vc, vc))

    kinetic_batched = jnp.broadcast_to(kinetic_matrix, (kl, radial, radial))

    def to_radial_columns(x):
        blocks = jnp.transpose(x.reshape(kl, rl, n, mb), (2, 0, 1, 3))
        got = lax.all_to_all(blocks, "rad", 0, 0, tiled=True).reshape(n, kl, rl, mb)
        return jnp.transpose(got, (1, 0, 2, 3)).reshape(kl, radial, mb)

    def to_radial_rows(y, companion=None):
        blocks = jnp.transpose(y.reshape(kl, n, rl, mb), (1, 0, 2, 3))
        got = lax.all_to_all(blocks, "rad", 0, 0, tiled=True).reshape(n, kl, rl, mb)
        if companion is not None:
            companion, got = lax.optimization_barrier((companion, got))
        return jnp.transpose(got, (1, 2, 0, 3)).reshape(kl, rl, vc, cc), companion

    def kinetic(columns):
        return jnp.einsum(
            "krs,ksm->krm",
            kinetic_batched,
            columns,
            precision=PRECISE,
            preferred_element_type=jnp.float32,
        )

    def local_part(current):
        angles = jnp.dot(
            current.reshape(-1, cc), transform.T, precision=PRECISE,
            preferred_element_type=jnp.float32,
        )
        angles = jnp.einsum(
            "buv,bva->bua",
            vib_batched,
            angles.reshape(kl * rl, vc, -1),
            precision=PRECISE,
            preferred_element_type=jnp.float32,
        )
        angles = angles.reshape(kl, rl, vc, -1) * potential[None, :, None, :]
        angular = jnp.dot(
            angles.reshape(-1, angles.shape[3]),
            transform,
            precision=PRECISE,
            preferred_element_type=jnp.float32,
        )
        weighted = coriolis[:, None, None, :] * current
        from_above = shifted(current[:1], "hel", -1)
        from_below = shifted(weighted[-1:], "hel", 1)
        upper_side = jnp.concatenate([current[1:], from_above], axis=0)
        lower_side = jnp.concatenate([from_below, weighted[:-1]], axis=0)
        return (
            angular.reshape(current.shape) + vib_energy[None, None, :, None] * current
        ) + radial_local[None, :, None, None] * (
            coriolis[:, None, None, :] * upper_side + lower_side
        )

    damp_columns = damping[None, :, None]
    earlier = prev_vector
    current = curr_vector
    columns = to_radial_columns(current)
    for iteration in range(STEPS - 1):
        rest = damp_full * (2.0 * local_part(current) - damp_full * earlier)
        following_columns = damp_columns * (2.0 * kinetic(columns)) + to_radial_columns(rest)
        earlier = current
        current, _ = to_radial_rows(following_columns)
        columns = following_columns
    kinetic_image, local_image = to_radial_rows(kinetic(columns), local_part(current))
    image = kinetic_image + local_image
    current = damp_full * (2.0 * image - damp_full * earlier)

    hel_index = lax.axis_index("hel")
    interp = interp_matrix(stencil, interp_weights, radial)
    qq = interp.shape[0]
    qb = qq // nh
    turn = jnp.arange(nh, dtype=jnp.int32)
    q_rows = (lax.rem(hel_index + turn, nh)[:, None] * qb + jnp.arange(qb)[None, :]).reshape(-1)
    interp_turned = jnp.broadcast_to(interp[q_rows], (kl, qq, radial))
    k_cols = (lax.rem(hel_index - turn + nh, nh)[:, None] * kl + jnp.arange(kl)[None, :]).reshape(-1)
    j_rows = (lax.rem(hel_index + turn, nh)[:, None] * kl + jnp.arange(kl)[None, :]).reshape(-1)
    frame_turned = frame_rotation[j_rows][:, k_cols]

    def hel_shift(x, d):
        if d == 0:
            return x
        return lax.ppermute(x, "hel", [(i, (i + d) % nh) for i in range(nh)])

    if vc % 8 == 0:
        sizes = [vc // 8] + [vc // 4] * 3 + [vc // 8]
    else:
        sizes = [vc]
    bounds = [sum(sizes[:i]) for i in range(len(sizes) + 1)]
    results = []

    def forward(placed):
        width = placed.shape[2]
        arrived = [hel_shift(placed[:, d * qb:(d + 1) * qb], d) for d in range(nh)]
        gathered = jnp.stack(arrived, axis=0)
        return jnp.dot(
            frame_turned,
            gathered.reshape(nh * kl, qb * width),
            precision=PRECISE,
            preferred_element_type=jnp.float32,
        ).reshape(nh, kl, qb, width)

    def backward(turned):
        vs = turned.shape[3] // cb
        back = [hel_shift(turned[e], e) for e in range(nh)]
        blocks = []
        for block in range(nh):
            source = lax.rem(hel_index - block + nh, nh)
            pick = back[0]
            for e in range(1, nh):
                pick = jnp.where(source == e, back[e], pick)
            blocks.append(pick)
        rotated = jnp.concatenate(blocks, axis=1)
        results.append(rotated.reshape(kl, qq, vs, cb))

    pending = None
    turning = None
    for lo, hi in zip(bounds[:-1], bounds[1:]):
        part = current[:, :, lo:hi, :]
        vs = hi - lo
        width = vs * cb
        if pending is not None:
            if turning is not None:
                pending, turning, part = lax.optimization_barrier((pending, turning, part))
                backward(turning)
            else:
                pending, part = lax.optimization_barrier((pending, part))
            turning = forward(pending)
        chans = jnp.transpose(part.reshape(kl, rl, vs, n, cb), (3, 0, 1, 2, 4))
        got = lax.all_to_all(chans.reshape(n, kl, rl, width), "rad", 0, 0, tiled=True)
        radial_block = jnp.transpose(got.reshape(n, kl, rl, width), (1, 0, 2, 3)).reshape(
            kl, radial, width
        )
        pending = jnp.einsum(
            "kqr,krm->kqm",
            interp_turned,
            radial_block,
            precision=PRECISE,
            preferred_element_type=jnp.float32,
        )
    if turning is not None:
        backward(turning)
    backward(forward(pending))
    product_amp = jnp.concatenate(results, axis=2)
    return (current, product_amp)


def solution(mesh):
    in_specs = (
        P("hel", "rad", None, None),
        P("hel", "rad", None, None),
        P(),
        P(),
        P(),
        P(),
        P("rad", None),
        P(),
        P(),
        P("hel", None),
        P(),
        P(),
        P(),
        P(),
        P(),
    )
    out_specs = (P("hel", "rad", None, None), P("hel", None, None, "rad"))
    return jax.shard_map(shards, mesh=mesh, in_specs=in_specs, out_specs=out_specs, check_vma=False)
```

```python
import jax
import jax.numpy as jnp
from jax import lax
from jax.sharding import PartitionSpec as P

STEPS = 2
PRECISE = lax.Precision.HIGHEST


def shifted(block, axis, distance):
    devices = range(lax.axis_size(axis))
    route = [(i - distance, i) for i in devices if i - distance in devices]
    return lax.ppermute(block, axis, route)


def angular_matrix(basis_first, basis_second, chan_table):
    levels = basis_first.shape[1]
    level_grid = jnp.arange(levels, dtype=jnp.int32)
    first_hot = (chan_table[None, :] // levels == level_grid[:, None]).astype(jnp.float32)
    second_hot = (chan_table[None, :] % levels == level_grid[:, None]).astype(jnp.float32)
    first_part = jnp.dot(
        basis_first, first_hot, precision=PRECISE, preferred_element_type=jnp.float32
    )
    second_part = jnp.dot(
        basis_second, second_hot, precision=PRECISE, preferred_element_type=jnp.float32
    )
    return first_part * second_part


def interp_matrix(stencil, interp_weights, radial_count):
    offsets = jnp.arange(4, dtype=jnp.int32)
    points = jnp.arange(radial_count, dtype=jnp.int32)
    matches = (points[None, None, :] == (stencil[:, None] + offsets[None, :])[:, :, None]).astype(
        jnp.float32
    )
    return jnp.sum(matches * interp_weights[:, :, None], axis=1)


def shards(
    prev_vector,
    curr_vector,
    kinetic_matrix,
    basis_first,
    basis_second,
    chan_table,
    potential,
    vib_coupling,
    vib_energy,
    coriolis,
    radial_factor,
    damping,
    stencil,
    interp_weights,
    frame_rotation,
):
    kl, rl, vc, cc = curr_vector.shape
    n = lax.axis_size("rad")
    nh = lax.axis_size("hel")
    radial = rl * n
    mb = vc * cc // n
    cb = cc // n
    rad_index = lax.axis_index("rad")
    radial_local = lax.dynamic_slice_in_dim(radial_factor, rad_index * rl, rl)
    damping_local = lax.dynamic_slice_in_dim(damping, rad_index * rl, rl)
    damp_full = damping_local[None, :, None, None]
    transform = angular_matrix(basis_first, basis_second, chan_table)
    vib_batched = jnp.broadcast_to(vib_coupling, (kl * rl, vc, vc))

    kinetic_batched = jnp.broadcast_to(kinetic_matrix, (kl, radial, radial))

    def to_radial_columns(x):
        blocks = jnp.transpose(x.reshape(kl, rl, n, mb), (2, 0, 1, 3))
        got = lax.all_to_all(blocks, "rad", 0, 0, tiled=True).reshape(n, kl, rl, mb)
        return jnp.transpose(got, (1, 0, 2, 3)).reshape(kl, radial, mb)

    def to_radial_rows(y, companion=None):
        blocks = jnp.transpose(y.reshape(kl, n, rl, mb), (1, 0, 2, 3))
        got = lax.all_to_all(blocks, "rad", 0, 0, tiled=True).reshape(n, kl, rl, mb)
        if companion is not None:
            companion, got = lax.optimization_barrier((companion, got))
        return jnp.transpose(got, (1, 2, 0, 3)).reshape(kl, rl, vc, cc), companion

    def kinetic(columns):
        return jnp.einsum(
            "krs,ksm->krm",
            kinetic_batched,
            columns,
            precision=PRECISE,
            preferred_element_type=jnp.float32,
        )

    def local_part(current):
        angles = jnp.dot(
            current.reshape(-1, cc), transform.T, precision=PRECISE,
            preferred_element_type=jnp.float32,
        )
        angles = jnp.einsum(
            "buv,bva->bua",
            vib_batched,
            angles.reshape(kl * rl, vc, -1),
            precision=PRECISE,
            preferred_element_type=jnp.float32,
        )
        angles = angles.reshape(kl, rl, vc, -1) * potential[None, :, None, :]
        angular = jnp.dot(
            angles.reshape(-1, angles.shape[3]),
            transform,
            precision=PRECISE,
            preferred_element_type=jnp.float32,
        )
        weighted = coriolis[:, None, None, :] * current
        from_above = shifted(current[:1], "hel", -1)
        from_below = shifted(weighted[-1:], "hel", 1)
        upper_side = jnp.concatenate([current[1:], from_above], axis=0)
        lower_side = jnp.concatenate([from_below, weighted[:-1]], axis=0)
        return (
            angular.reshape(current.shape) + vib_energy[None, None, :, None] * current
        ) + radial_local[None, :, None, None] * (
            coriolis[:, None, None, :] * upper_side + lower_side
        )

    damp_columns = damping[None, :, None]
    earlier = prev_vector
    current = curr_vector
    columns = to_radial_columns(current)
    for iteration in range(STEPS - 1):
        rest = damp_full * (2.0 * local_part(current) - damp_full * earlier)
        following_columns = damp_columns * (2.0 * kinetic(columns)) + to_radial_columns(rest)
        earlier = current
        current, _ = to_radial_rows(following_columns)
        columns = following_columns
    kinetic_image, local_image = to_radial_rows(kinetic(columns), local_part(current))
    image = kinetic_image + local_image
    current = damp_full * (2.0 * image - damp_full * earlier)

    hel_index = lax.axis_index("hel")
    interp = interp_matrix(stencil, interp_weights, radial)
    qq = interp.shape[0]
    qb = qq // nh
    turn = jnp.arange(nh, dtype=jnp.int32)
    q_rows = (lax.rem(hel_index + turn, nh)[:, None] * qb + jnp.arange(qb)[None, :]).reshape(-1)
    interp_turned = jnp.broadcast_to(interp[q_rows], (kl, qq, radial))
    k_cols = (lax.rem(hel_index - turn + nh, nh)[:, None] * kl + jnp.arange(kl)[None, :]).reshape(-1)
    j_rows = (lax.rem(hel_index + turn, nh)[:, None] * kl + jnp.arange(kl)[None, :]).reshape(-1)
    frame_turned = frame_rotation[j_rows][:, k_cols]

    def hel_shift(x, d):
        if d == 0:
            return x
        return lax.ppermute(x, "hel", [(i, (i + d) % nh) for i in range(nh)])

    if vc % 8 == 0:
        sizes = [vc // 8, 3 * vc // 8, 3 * vc // 8, vc // 8]
    else:
        sizes = [vc]
    bounds = [sum(sizes[:i]) for i in range(len(sizes) + 1)]
    results = []

    def forward(placed):
        width = placed.shape[2]
        arrived = [hel_shift(placed[:, d * qb:(d + 1) * qb], d) for d in range(nh)]
        gathered = jnp.stack(arrived, axis=0)
        return jnp.dot(
            frame_turned,
            gathered.reshape(nh * kl, qb * width),
            precision=PRECISE,
            preferred_element_type=jnp.float32,
        ).reshape(nh, kl, qb, width)

    def backward(turned):
        vs = turned.shape[3] // cb
        back = [hel_shift(turned[e], e) for e in range(nh)]
        blocks = []
        for block in range(nh):
            source = lax.rem(hel_index - block + nh, nh)
            pick = back[0]
            for e in range(1, nh):
                pick = jnp.where(source == e, back[e], pick)
            blocks.append(pick)
        rotated = jnp.concatenate(blocks, axis=1)
        results.append(rotated.reshape(kl, qq, vs, cb))

    pending = None
    turning = None
    for lo, hi in zip(bounds[:-1], bounds[1:]):
        part = current[:, :, lo:hi, :]
        vs = hi - lo
        width = vs * cb
        if pending is not None:
            if turning is not None:
                pending, turning, part = lax.optimization_barrier((pending, turning, part))
                backward(turning)
            else:
                pending, part = lax.optimization_barrier((pending, part))
            turning = forward(pending)
        chans = jnp.transpose(part.reshape(kl, rl, vs, n, cb), (3, 0, 1, 2, 4))
        got = lax.all_to_all(chans.reshape(n, kl, rl, width), "rad", 0, 0, tiled=True)
        radial_block = jnp.transpose(got.reshape(n, kl, rl, width), (1, 0, 2, 3)).reshape(
            kl, radial, width
        )
        pending = jnp.einsum(
            "kqr,krm->kqm",
            interp_turned,
            radial_block,
            precision=PRECISE,
            preferred_element_type=jnp.float32,
        )
    if turning is not None:
        backward(turning)
    backward(forward(pending))
    product_amp = jnp.concatenate(results, axis=2)
    return (current, product_amp)


def solution(mesh):
    in_specs = (
        P("hel", "rad", None, None),
        P("hel", "rad", None, None),
        P(),
        P(),
        P(),
        P(),
        P("rad", None),
        P(),
        P(),
        P("hel", None),
        P(),
        P(),
        P(),
        P(),
        P(),
    )
    out_specs = (P("hel", "rad", None, None), P("hel", None, None, "rad"))
    return jax.shard_map(shards, mesh=mesh, in_specs=in_specs, out_specs=out_specs, check_vma=False)
```

```python
import jax
import jax.numpy as jnp
from jax import lax
from jax.sharding import PartitionSpec as P

STEPS = 2
PRECISE = lax.Precision.HIGHEST


def shifted(block, axis, distance):
    devices = range(lax.axis_size(axis))
    route = [(i - distance, i) for i in devices if i - distance in devices]
    return lax.ppermute(block, axis, route)


def angular_matrix(basis_first, basis_second, chan_table):
    levels = basis_first.shape[1]
    level_grid = jnp.arange(levels, dtype=jnp.int32)
    first_hot = (chan_table[None, :] // levels == level_grid[:, None]).astype(jnp.float32)
    second_hot = (chan_table[None, :] % levels == level_grid[:, None]).astype(jnp.float32)
    first_part = jnp.dot(
        basis_first, first_hot, precision=PRECISE, preferred_element_type=jnp.float32
    )
    second_part = jnp.dot(
        basis_second, second_hot, precision=PRECISE, preferred_element_type=jnp.float32
    )
    return first_part * second_part


def interp_matrix(stencil, interp_weights, radial_count):
    offsets = jnp.arange(4, dtype=jnp.int32)
    points = jnp.arange(radial_count, dtype=jnp.int32)
    matches = (points[None, None, :] == (stencil[:, None] + offsets[None, :])[:, :, None]).astype(
        jnp.float32
    )
    return jnp.sum(matches * interp_weights[:, :, None], axis=1)


def shards(
    prev_vector,
    curr_vector,
    kinetic_matrix,
    basis_first,
    basis_second,
    chan_table,
    potential,
    vib_coupling,
    vib_energy,
    coriolis,
    radial_factor,
    damping,
    stencil,
    interp_weights,
    frame_rotation,
):
    kl, rl, vc, cc = curr_vector.shape
    n = lax.axis_size("rad")
    nh = lax.axis_size("hel")
    radial = rl * n
    mb = vc * cc // n
    cb = cc // n
    rad_index = lax.axis_index("rad")
    radial_local = lax.dynamic_slice_in_dim(radial_factor, rad_index * rl, rl)
    damping_local = lax.dynamic_slice_in_dim(damping, rad_index * rl, rl)
    damp_full = damping_local[None, :, None, None]
    transform = angular_matrix(basis_first, basis_second, chan_table)
    vib_batched = jnp.broadcast_to(vib_coupling, (kl * rl, vc, vc))

    kinetic_batched = jnp.broadcast_to(kinetic_matrix, (kl, radial, radial))

    def to_radial_columns(x):
        blocks = jnp.transpose(x.reshape(kl, rl, n, mb), (2, 0, 1, 3))
        got = lax.all_to_all(blocks, "rad", 0, 0, tiled=True).reshape(n, kl, rl, mb)
        return jnp.transpose(got, (1, 0, 2, 3)).reshape(kl, radial, mb)

    def to_radial_rows(y, companion=None):
        blocks = jnp.transpose(y.reshape(kl, n, rl, mb), (1, 0, 2, 3))
        got = lax.all_to_all(blocks, "rad", 0, 0, tiled=True).reshape(n, kl, rl, mb)
        if companion is not None:
            companion, got = lax.optimization_barrier((companion, got))
        return jnp.transpose(got, (1, 2, 0, 3)).reshape(kl, rl, vc, cc), companion

    def kinetic(columns):
        return jnp.einsum(
            "krs,ksm->krm",
            kinetic_batched,
            columns,
            precision=PRECISE,
            preferred_element_type=jnp.float32,
        )

    def local_part(current):
        angles = jnp.dot(
            current.reshape(-1, cc), transform.T, precision=PRECISE,
            preferred_element_type=jnp.float32,
        )
        angles = jnp.einsum(
            "buv,bva->bua",
            vib_batched,
            angles.reshape(kl * rl, vc, -1),
            precision=PRECISE,
            preferred_element_type=jnp.float32,
        )
        angles = angles.reshape(kl, rl, vc, -1) * potential[None, :, None, :]
        angular = jnp.dot(
            angles.reshape(-1, angles.shape[3]),
            transform,
            precision=PRECISE,
            preferred_element_type=jnp.float32,
        )
        weighted = coriolis[:, None, None, :] * current
        from_above = shifted(current[:1], "hel", -1)
        from_below = shifted(weighted[-1:], "hel", 1)
        upper_side = jnp.concatenate([current[1:], from_above], axis=0)
        lower_side = jnp.concatenate([from_below, weighted[:-1]], axis=0)
        return (
            angular.reshape(current.shape) + vib_energy[None, None, :, None] * current
        ) + radial_local[None, :, None, None] * (
            coriolis[:, None, None, :] * upper_side + lower_side
        )

    damp_columns = damping[None, :, None]
    earlier = prev_vector
    current = curr_vector
    columns = to_radial_columns(current)
    for iteration in range(STEPS - 1):
        rest = damp_full * (2.0 * local_part(current) - damp_full * earlier)
        following_columns = damp_columns * (2.0 * kinetic(columns)) + to_radial_columns(rest)
        earlier = current
        current, _ = to_radial_rows(following_columns)
        columns = following_columns
    kinetic_image, local_image = to_radial_rows(kinetic(columns), local_part(current))
    image = kinetic_image + local_image
    current = damp_full * (2.0 * image - damp_full * earlier)

    hel_index = lax.axis_index("hel")
    interp = interp_matrix(stencil, interp_weights, radial)
    qq = interp.shape[0]
    qb = qq // nh
    turn = jnp.arange(nh, dtype=jnp.int32)
    q_rows = (lax.rem(hel_index + turn, nh)[:, None] * qb + jnp.arange(qb)[None, :]).reshape(-1)
    interp_turned = jnp.broadcast_to(interp[q_rows], (kl, qq, radial))
    k_cols = (lax.rem(hel_index - turn + nh, nh)[:, None] * kl + jnp.arange(kl)[None, :]).reshape(-1)
    j_rows = (lax.rem(hel_index + turn, nh)[:, None] * kl + jnp.arange(kl)[None, :]).reshape(-1)
    frame_turned = frame_rotation[j_rows][:, k_cols]

    def hel_shift(x, d):
        if d == 0:
            return x
        return lax.ppermute(x, "hel", [(i, (i + d) % nh) for i in range(nh)])

    if vc % 8 == 0:
        sizes = [vc // 8] * 2 + [vc // 4] * 2 + [vc // 8] * 2
    else:
        sizes = [vc]
    bounds = [sum(sizes[:i]) for i in range(len(sizes) + 1)]
    results = []

    def finish(placed):
        vs = placed.shape[2] // cb
        width = vs * cb
        arrived = [hel_shift(placed[:, d * qb:(d + 1) * qb], d) for d in range(nh)]
        gathered = jnp.stack(arrived, axis=0)
        turned = jnp.dot(
            frame_turned,
            gathered.reshape(nh * kl, qb * width),
            precision=PRECISE,
            preferred_element_type=jnp.float32,
        ).reshape(nh, kl, qb, width)
        back = [hel_shift(turned[e], e) for e in range(nh)]
        blocks = []
        for block in range(nh):
            source = lax.rem(hel_index - block + nh, nh)
            pick = back[0]
            for e in range(1, nh):
                pick = jnp.where(source == e, back[e], pick)
            blocks.append(pick)
        rotated = jnp.concatenate(blocks, axis=1)
        results.append(rotated.reshape(kl, qq, vs, cb))

    pending = None
    for lo, hi in zip(bounds[:-1], bounds[1:]):
        part = current[:, :, lo:hi, :]
        vs = hi - lo
        width = vs * cb
        if pending is not None:
            pending, part = lax.optimization_barrier((pending, part))
            finish(pending)
        chans = jnp.transpose(part.reshape(kl, rl, vs, n, cb), (3, 0, 1, 2, 4))
        got = lax.all_to_all(chans.reshape(n, kl, rl, width), "rad", 0, 0, tiled=True)
        radial_block = jnp.transpose(got.reshape(n, kl, rl, width), (1, 0, 2, 3)).reshape(
            kl, radial, width
        )
        placed = jnp.einsum(
            "kqr,krm->kqm",
            interp_turned,
            radial_block,
            precision=PRECISE,
            preferred_element_type=jnp.float32,
        )
        pending = placed
    finish(pending)
    product_amp = jnp.concatenate(results, axis=2)
    return (current, product_amp)


def solution(mesh):
    in_specs = (
        P("hel", "rad", None, None),
        P("hel", "rad", None, None),
        P(),
        P(),
        P(),
        P(),
        P("rad", None),
        P(),
        P(),
        P("hel", None),
        P(),
        P(),
        P(),
        P(),
        P(),
    )
    out_specs = (P("hel", "rad", None, None), P("hel", None, None, "rad"))
    return jax.shard_map(shards, mesh=mesh, in_specs=in_specs, out_specs=out_specs, check_vma=False)
```
